256 devices in a mesh: ctx: 32 (over z, x), dp: 8 (over y, core).
Axes of the slice: x: 4, y: 4, z: 8, core: 2. Of those that a mesh axis runs over, the one named last changes fastest.
Arguments:
- layer_input: bfloat16 [8, 4096, 5376], P('dp', 'ctx'), may hold values from -12 to 12
- query_states: bfloat16 [8, 4096, 2048], P('dp', 'ctx'), may hold values from -6 to 6
- key_states: bfloat16 [8, 4096, 1024], P('dp', 'ctx'), may hold values from -6 to 6
- value_state_rows: bfloat16 [8, 4096, 1024], P('dp', 'ctx'), may hold values from -6 to 6
- grad_out: bfloat16 [8, 4096, 2048], P('dp', 'ctx'), may hold values from -180 to 180
- segments: int32 [8, 4096], P('dp', 'ctx'), may hold values from 0 to 7, never falling along the last dimension, each value on 1 to 2048 neighbouring positions
- master: float32 [5376, 1024], P(('ctx', 'dp')), may hold values from -0.078125 to 0.078125
- first_moment_value: float32 [5376, 1024], P(('ctx', 'dp')), may hold values from -0.0024 to 0.0024
- second_moment_value: float32 [5376, 1024], P(('ctx', 'dp')), may hold values from 1e-08 to 1e-06
Outputs:
- query_gradient: bfloat16 [8, 4096, 2048], P('dp', 'ctx')
- key_gradient: bfloat16 [8, 4096, 1024], P('dp', 'ctx')
- value_gradient: bfloat16 [8, 4096, 1024], P('dp', 'ctx')
- new_master: float32 [5376, 1024], P(('ctx', 'dp'))
- new_first: float32 [5376, 1024], P(('ctx', 'dp'))
- new_second: float32 [5376, 1024], P(('ctx', 'dp'))
- new_weight: bfloat16 [5376, 1024], P('ctx')
The draws below stay inside these ranges and needn't reach their ends.
Inputs may be any that keep to these rules, and one draw needn't show every extreme that they name: `segments`: segment numbers never fall along a sequence; each document holds 1 to 2048 tokens and one holds exactly 2048.
All inputs are finite; a program needn't handle non-finite values.
Results may differ from the reference program's by a relative error of at most 0.01.
The reference program's roundings to bfloat16 on the way count: a program that leaves them out, or rounds other values in their place, can miss the bound.
Values may be sent and summed in bfloat16 or wider, within the bound.
No kernel may reach another device: no remote copies, remote signals or barrier semaphores. Data moves between devices by JAX's collectives and lax.ppermute only.
A program may use at most 128 MiB of HBM per device.

```python
import math
import jax
import jax.numpy as jnp
import numpy as np
from jax import lax

MODEL_WIDTH = 5376
QUERY_HEADS = 16
KEY_VALUE_HEADS = 8
HEAD_SIZE = 128
WINDOW = 1024
TOK_DEV = 128
SEQUENCE_COUNT = 8
SEQUENCE_TOKENS = 4096
SEGS = 8
DOC_MOST = 2048
N_CTX = 32


def drawn_draw(key):
    base_offset = jax.random.fold_in(key, 17)
    query_sample = jax.random.normal(jax.random.fold_in(base_offset, 1), (SEQUENCE_COUNT, SEQUENCE_TOKENS, QUERY_HEADS, HEAD_SIZE), jnp.float32)
    key_sample = jax.random.normal(jax.random.fold_in(base_offset, 2), (SEQUENCE_COUNT, SEQUENCE_TOKENS, KEY_VALUE_HEADS, HEAD_SIZE), jnp.float32)
    query_sample = jnp.clip(query_sample, -6.0, 6.0)
    key_sample = jnp.clip(key_sample, -6.0, 6.0)
    return (query_sample.reshape(SEQUENCE_COUNT, SEQUENCE_TOKENS, QUERY_HEADS * HEAD_SIZE), key_sample.reshape(SEQUENCE_COUNT, SEQUENCE_TOKENS, KEY_VALUE_HEADS * HEAD_SIZE))


def draw_query_states(key, part):
    query_sample, key_sample = drawn_draw(key)
    return query_sample.astype(jnp.bfloat16)


def draw_key_states(key, part):
    query_sample, key_sample = drawn_draw(key)
    return key_sample.astype(jnp.bfloat16)


def draw_layer_input(key, part):
    block_count = SEQUENCE_TOKENS // TOK_DEV
    feature_block = MODEL_WIDTH // block_count
    pairing = jax.random.permutation(jax.random.fold_in(key, 31), block_count)
    token_block = jnp.arange(SEQUENCE_TOKENS) // TOK_DEV
    feature_index = jnp.arange(MODEL_WIDTH) // feature_block
    paired_mask = pairing[token_block][:, None] == feature_index[None, :]
    spike_factor = jnp.where(paired_mask, 3.0, 1.0).astype(jnp.float32)
    feature_mean = jnp.clip(jax.random.normal(jax.random.fold_in(key, 32), (MODEL_WIDTH,), jnp.float32), -2.5, 2.5)
    array_shape = (SEQUENCE_COUNT, SEQUENCE_TOKENS, MODEL_WIDTH)
    base_values = jnp.clip(jax.random.normal(jax.random.fold_in(key, 34), array_shape, jnp.float32), -4.0, 4.0)
    mean_weight = 1.1 * SEQUENCE_TOKENS ** (-0.5)
    drawn_values = base_values * spike_factor[None, :, :] + mean_weight * feature_mean[None, None, :]
    return jnp.clip(drawn_values, -12.0, 12.0).astype(jnp.bfloat16)


def draw_grad_out(key, part):
    array_shape = (SEQUENCE_COUNT, SEQUENCE_TOKENS, QUERY_HEADS * HEAD_SIZE)
    feature_mean = jnp.clip(jax.random.normal(jax.random.fold_in(key, 41), (QUERY_HEADS * HEAD_SIZE,), jnp.float32), -2.5, 2.5)
    base_values = jnp.clip(30.0 * jax.random.normal(jax.random.fold_in(key, 43), array_shape, jnp.float32), -150.0, 150.0)
    mean_weight = 6.0
    drawn_values = base_values + mean_weight * feature_mean[None, None, :]
    return jnp.clip(drawn_values, -180.0, 180.0).astype(jnp.bfloat16)


def steps_of(key, extent, pieces, least, largest):
    def one(dim, parts):
        steps = jax.random.uniform(jax.random.fold_in(jax.random.fold_in(key, 6), dim), (parts,), jnp.float32, least / len(pieces), largest / len(pieces))
        return jnp.repeat(jnp.exp(steps), extent[dim] // parts).reshape((-1,) + (1,) * (len(extent) - dim - 1))

    gain = one(*pieces[0])
    for cut in pieces[1:]:
        gain = gain * one(*cut)
    return gain


def profile(count, total, reach, lean):
    loads = [(1 << 20) // math.isqrt(standing ** lean) + 1 for standing in range(2, count + 1)]
    spare, counts = total - reach - (count - 1), [1] * (count - 1)
    while spare > 0:
        free = [i for i in range(count - 1) if counts[i] < reach]
        mass, remaining = sum([loads[i] for i in free]), spare
        for i in free:
            addition = min(reach - counts[i], max(1, remaining * loads[i] // mass), spare)
            counts[i] = counts[i] + addition
            spare = spare - addition
    return np.array([reach] + counts)


def ragged(stream_key, number_of, total, bound, skew):
    if number_of == 2:
        one = jax.random.randint(stream_key, (), max(1, total - bound), min(bound, total - 1) + 1)
        return jnp.stack([one, total - one])
    tallies = jnp.asarray(profile(number_of, total, bound, skew), jnp.int32)
    couples = (number_of - 1) // 2
    source_of, sink = tallies[1:1 + 2 * couples:2], tallies[2:2 + 2 * couples:2]
    room = jnp.minimum(source_of - 1, bound - sink)
    shifted = jax.random.randint(jax.random.fold_in(stream_key, 1), (couples,), 0, 1 << 20) % (room + 1)
    tallies = tallies.at[1:1 + 2 * couples:2].set(source_of - shifted).at[2:2 + 2 * couples:2].set(sink + shifted)
    return tallies[jax.random.permutation(jax.random.fold_in(stream_key, 2), number_of)]


def bell_draw(rng, dims, width, limit, shards=(), kind=jnp.bfloat16):
    result = jax.random.normal(rng, dims, jnp.float32) * width
    if len(shards) > 0:
        result = steps_of(rng, dims, shards, -0.22, 0.18) * result
    return jnp.clip(result, min=-limit, max=limit).astype(kind)


def setup_inputs(seed: int = 0) -> dict:
    arg_keys = jax.random.split(jax.random.key(seed), 10)
    return {
        "layer_input": draw_layer_input(jax.random.fold_in(arg_keys[9], 71), 0),
        "query_states": draw_query_states(jax.random.fold_in(arg_keys[9], 71), 0),
        "key_states": draw_key_states(jax.random.fold_in(arg_keys[9], 71), 0),
        "value_state_rows": bell_draw(arg_keys[3], (SEQUENCE_COUNT, SEQUENCE_TOKENS, KEY_VALUE_HEADS * HEAD_SIZE), 1.0, 6.0, ((0, 8), (1, 32))),
        "grad_out": draw_grad_out(jax.random.fold_in(arg_keys[9], 71), 0),
        "segments": jax.vmap(lambda own: jnp.searchsorted(jnp.cumsum(ragged(own, SEGS, SEQUENCE_TOKENS, DOC_MOST, 0)), jnp.arange(SEQUENCE_TOKENS), side="right"))(jax.random.split(arg_keys[5], SEQUENCE_COUNT)).reshape((SEQUENCE_COUNT, SEQUENCE_TOKENS)).astype(jnp.int32),
        "master": bell_draw(arg_keys[6], (MODEL_WIDTH, KEY_VALUE_HEADS * HEAD_SIZE), MODEL_WIDTH ** -0.5, 0.078125, ((0, 256),), jnp.float32),
        "first_moment_value": bell_draw(arg_keys[7], (MODEL_WIDTH, KEY_VALUE_HEADS * HEAD_SIZE), 0.0004, 0.0024, ((0, 256),), jnp.float32),
        "second_moment_value": jnp.clip(jnp.exp(math.log(9.999999974752427e-07) - 4.6051702 * jax.random.uniform(arg_keys[8], (MODEL_WIDTH, KEY_VALUE_HEADS * HEAD_SIZE), jnp.float32) ** steps_of(arg_keys[8], (MODEL_WIDTH, KEY_VALUE_HEADS * HEAD_SIZE), ((0, 256),), -0.2, 0.2)), 9.99999993922529e-09, 9.999999974752427e-07),
    }


query_scale = 168.0 ** (-0.5)
masked_score = -1e+30
clip_norm = 1.0
beta_first = 0.9
beta_second = 0.95
learn_rate = 0.001
decay_rate = 0.1
adam_eps = 1e-08
correct_first = 0.9999734386011124
correct_second = 0.994079470779666

def low_round(values_in):
    rounded = values_in.astype(jnp.bfloat16)
    rounded = lax.optimization_barrier(rounded)
    return rounded.astype(jnp.float32)

def attend(query_row_block, key_row_block, value_row_block, gradient_rows, seg_query, seg_key, index_query, index_key):
    shard_length = query_row_block.shape[0]
    extent_rows = key_row_block.shape[0]
    heads_ratio = QUERY_HEADS // KEY_VALUE_HEADS
    query_four_axes = query_row_block.reshape(shard_length, KEY_VALUE_HEADS, heads_ratio, HEAD_SIZE).astype(jnp.float32)
    gradient_four_axes = gradient_rows.reshape(shard_length, KEY_VALUE_HEADS, heads_ratio, HEAD_SIZE).astype(jnp.float32)
    key_three_axes = key_row_block.reshape(extent_rows, KEY_VALUE_HEADS, HEAD_SIZE).astype(jnp.float32)
    value_three_axes = value_row_block.reshape(extent_rows, KEY_VALUE_HEADS, HEAD_SIZE).astype(jnp.float32)
    scores = jnp.einsum('tgrd,egd->grte', query_four_axes, key_three_axes) * query_scale
    offset = index_query[:, None] - index_key[None, :]
    allowed = (seg_query[:, None] == seg_key[None, :]) & (offset >= 0) & (offset < WINDOW) & (index_key[None, :] >= 0)
    scores = jnp.where(allowed, scores, masked_score)
    row_max = lax.optimization_barrier(jnp.max(scores, axis=-1, keepdims=True))
    weights = jnp.exp(scores - row_max)
    probabilities = weights / lax.optimization_barrier(jnp.sum(weights, axis=-1, keepdims=True))
    probs_low = low_round(probabilities)
    attn_out = jnp.einsum('grte,egd->tgrd', probs_low, value_three_axes)
    row_delta = lax.optimization_barrier(jnp.sum(gradient_four_axes * attn_out, axis=-1))
    grad_probs = jnp.einsum('tgrd,egd->grte', gradient_four_axes, value_three_axes)
    grad_scores = probabilities * (grad_probs - jnp.transpose(row_delta, (1, 2, 0))[..., None])
    scores_low = low_round(grad_scores)
    query_gradient = jnp.einsum('grte,egd->tgrd', scores_low, key_three_axes) * query_scale
    query_gradient = query_gradient.astype(jnp.bfloat16).reshape(shard_length, QUERY_HEADS * HEAD_SIZE)
    key_gradient = jnp.einsum('grte,tgrd->egd', scores_low, query_four_axes) * query_scale
    value_gradient = jnp.einsum('grte,tgrd->egd', probs_low, gradient_four_axes)
    return (query_gradient, key_gradient.reshape(extent_rows, KEY_VALUE_HEADS * HEAD_SIZE), value_gradient.reshape(extent_rows, KEY_VALUE_HEADS * HEAD_SIZE))

def reference(layer_input, query_states, key_states, value_state_rows, grad_out, segments, master, first_moment_value, second_moment_value):
    shard_length = TOK_DEV
    peer_count = min(WINDOW // TOK_DEV, N_CTX - 1)
    front_len = peer_count * shard_length
    extent_rows = front_len + shard_length
    key_value_width = KEY_VALUE_HEADS * HEAD_SIZE

    def one_sequence(packed):
        query_seq, key_seq, value_seq, grad_seq, seg_seq = packed
        key_pad = jnp.concatenate([jnp.zeros((front_len, key_value_width), key_seq.dtype), key_seq], axis=0)
        value_pad = jnp.concatenate([jnp.zeros((front_len, key_value_width), value_seq.dtype), value_seq], axis=0)
        seg_pad = jnp.concatenate([jnp.full((front_len,), -1, jnp.int32), seg_seq.astype(jnp.int32)], axis=0)

        def block(carried, shard_id):
            key_acc, value_acc = carried
            row_start = (shard_id * shard_length).astype(jnp.int32)
            query_row_block = lax.dynamic_slice_in_dim(query_seq, row_start, shard_length, 0)
            gradient_rows = lax.dynamic_slice_in_dim(grad_seq, row_start, shard_length, 0)
            seg_query = lax.dynamic_slice_in_dim(seg_seq.astype(jnp.int32), row_start, shard_length, 0)
            key_row_block = lax.dynamic_slice_in_dim(key_pad, row_start, extent_rows, 0)
            value_row_block = lax.dynamic_slice_in_dim(value_pad, row_start, extent_rows, 0)
            seg_key = lax.dynamic_slice_in_dim(seg_pad, row_start, extent_rows, 0)
            index_query = row_start + jnp.arange(shard_length, dtype=jnp.int32)
            index_key = row_start - front_len + jnp.arange(extent_rows, dtype=jnp.int32)
            query_gradient, key_gradient, value_gradient = attend(query_row_block, key_row_block, value_row_block, gradient_rows, seg_query, seg_key, index_query, index_key)
            merged_key = jnp.concatenate([low_round(key_gradient[:front_len]), key_gradient[front_len:]], axis=0)
            merged_value = jnp.concatenate([low_round(value_gradient[:front_len]), value_gradient[front_len:]], axis=0)
            key_acc = lax.dynamic_update_slice_in_dim(key_acc, lax.dynamic_slice_in_dim(key_acc, row_start, extent_rows, 0) + merged_key, row_start, 0)
            value_acc = lax.dynamic_update_slice_in_dim(value_acc, lax.dynamic_slice_in_dim(value_acc, row_start, extent_rows, 0) + merged_value, row_start, 0)
            return ((key_acc, value_acc), query_gradient)
        zero_acc = jnp.zeros((front_len + SEQUENCE_TOKENS, key_value_width), jnp.float32)
        (key_acc, value_acc), query_blocks = lax.scan(block, (zero_acc, zero_acc), jnp.arange(N_CTX, dtype=jnp.int32))
        return (query_blocks.reshape(SEQUENCE_TOKENS, QUERY_HEADS * HEAD_SIZE), key_acc[front_len:].astype(jnp.bfloat16), value_acc[front_len:].astype(jnp.bfloat16))
    query_gradient, key_gradient, value_gradient = lax.map(one_sequence, (query_states, key_states, value_state_rows, grad_out, segments))
    flat_input = layer_input.reshape(SEQUENCE_COUNT * SEQUENCE_TOKENS, MODEL_WIDTH)
    flat_value = value_gradient.reshape(SEQUENCE_COUNT * SEQUENCE_TOKENS, key_value_width)
    weight_grad = jnp.dot(flat_input.T, flat_value, preferred_element_type=jnp.float32)
    norm_total = jnp.sqrt(jnp.sum(weight_grad * weight_grad) + 1e-06)
    clipped = weight_grad * jnp.minimum(1.0, clip_norm / norm_total)
    new_first = beta_first * first_moment_value + (1.0 - beta_first) * clipped
    new_second = beta_second * second_moment_value + (1.0 - beta_second) * clipped * clipped
    step_dir = new_first / correct_first / (jnp.sqrt(new_second / correct_second) + adam_eps)
    new_master = master - learn_rate * (step_dir + decay_rate * master)
    new_weight = new_master.astype(jnp.bfloat16)
    return (query_gradient, key_gradient, value_gradient, new_master, new_first, new_second, new_weight)
```

```python
import jax
import jax.numpy as jnp
from jax import lax
from jax.sharding import Mesh
from jax.sharding import PartitionSpec as P

QUERY_HEADS = 16
KEY_VALUE_HEADS = 8
HEAD_SIZE = 128
WINDOW = 1024
Z_SIZE = 8

CTX = ("cz", "cx")

query_scale = 168.0 ** (-0.5)
masked_score = -1e30
clip_norm = 1.0
beta_first = 0.9
beta_second = 0.95
learn_rate = 0.001
decay_rate = 0.1
adam_eps = 1e-08
correct_first = 0.9999734386011124
correct_second = 0.994079470779666


def ctx_size():
    return lax.axis_size("cz") * lax.axis_size("cx")


def ctx_index():
    return lax.axis_index("cz") * lax.axis_size("cx") + lax.axis_index("cx")


def from_behind(x, by):
    count = ctx_size()
    pairs = [(i, i + by) for i in range(count) if 0 <= i + by < count]
    return lax.ppermute(x, CTX, pairs)


def attend(
    query_row_block,
    key_row_block,
    value_row_block,
    gradient_rows,
    seg_query,
    seg_key,
    index_query,
    index_key,
):
    shard_length = query_row_block.shape[0]
    extent_rows = key_row_block.shape[0]
    heads_ratio = QUERY_HEADS // KEY_VALUE_HEADS
    query_four_axes = query_row_block.reshape(shard_length, KEY_VALUE_HEADS, heads_ratio, HEAD_SIZE)
    gradient_four_axes = gradient_rows.reshape(
        shard_length, KEY_VALUE_HEADS, heads_ratio, HEAD_SIZE
    )
    key_three_axes = key_row_block.reshape(extent_rows, KEY_VALUE_HEADS, HEAD_SIZE)
    value_three_axes = value_row_block.reshape(extent_rows, KEY_VALUE_HEADS, HEAD_SIZE)
    scores = (
        jnp.einsum(
            "tgrd,egd->grte", query_four_axes, key_three_axes, preferred_element_type=jnp.float32
        )
        * query_scale
    )
    offset = index_query[:, None] - index_key[None, :]
    allowed = (
        (seg_query[:, None] == seg_key[None, :])
        & (offset >= 0)
        & (offset < WINDOW)
        & (index_key[None, :] >= 0)
    )
    scores = jnp.where(allowed, scores, masked_score)
    row_max = jnp.max(scores, axis=-1, keepdims=True)
    weights = jnp.exp(scores - row_max)
    probabilities = weights / jnp.sum(weights, axis=-1, keepdims=True)
    probs_low = probabilities.astype(jnp.bfloat16)
    attn_out = jnp.einsum(
        "grte,egd->tgrd", probs_low, value_three_axes, preferred_element_type=jnp.float32
    )
    row_delta = jnp.sum(gradient_four_axes.astype(jnp.float32) * attn_out, axis=-1)
    grad_probs = jnp.einsum(
        "tgrd,egd->grte", gradient_four_axes, value_three_axes, preferred_element_type=jnp.float32
    )
    grad_scores = probabilities * (grad_probs - jnp.transpose(row_delta, (1, 2, 0))[..., None])
    scores_low = grad_scores.astype(jnp.bfloat16)
    query_gradient = (
        jnp.einsum("grte,egd->tgrd", scores_low, key_three_axes, preferred_element_type=jnp.float32)
        * query_scale
    )
    query_gradient = query_gradient.astype(jnp.bfloat16).reshape(
        shard_length, QUERY_HEADS * HEAD_SIZE
    )
    key_gradient = (
        jnp.einsum(
            "grte,tgrd->egd", scores_low, query_four_axes, preferred_element_type=jnp.float32
        )
        * query_scale
    )
    value_gradient = jnp.einsum(
        "grte,tgrd->egd", probs_low, gradient_four_axes, preferred_element_type=jnp.float32
    )
    return (
        query_gradient,
        key_gradient.reshape(extent_rows, KEY_VALUE_HEADS * HEAD_SIZE),
        value_gradient.reshape(extent_rows, KEY_VALUE_HEADS * HEAD_SIZE),
    )


def shards(
    layer_input,
    query_states,
    key_states,
    value_state_rows,
    grad_out,
    segments,
    master,
    first_moment_value,
    second_moment_value,
):
    shard_length = query_states.shape[1]
    kv_width = key_states.shape[2]
    peer_count = min(WINDOW // shard_length, ctx_size() - 1)
    front_len = peer_count * shard_length
    position = ctx_index() * shard_length

    seg_all = lax.all_gather(segments[0], CTX, axis=0, tiled=True)
    seg_pad = jnp.concatenate([jnp.full((front_len,), -1, jnp.int32), seg_all], axis=0)
    seg_key = lax.dynamic_slice_in_dim(seg_pad, position, front_len + shard_length, 0)
    seg_query = segments[0]

    own_kv = jnp.concatenate([key_states[0], value_state_rows[0]], axis=1)
    incoming = [from_behind(own_kv, distance) for distance in range(peer_count, 0, -1)]
    kv_rows = jnp.concatenate(incoming + [own_kv], axis=0)
    key_row_block = kv_rows[:, :kv_width]
    value_row_block = kv_rows[:, kv_width:]
    index_query = position + jnp.arange(shard_length, dtype=jnp.int32)
    index_key = position - front_len + jnp.arange(front_len + shard_length, dtype=jnp.int32)
    query_gradient, key_gradient, value_gradient = attend(
        query_states[0],
        key_row_block,
        value_row_block,
        grad_out[0],
        seg_query,
        seg_key,
        index_query,
        index_key,
    )
    key_sum = key_gradient[front_len:]
    value_sum = value_gradient[front_len:]
    for distance in range(1, peer_count + 1):
        lower = (peer_count - distance) * shard_length
        part = jnp.concatenate(
            [
                key_gradient[lower : lower + shard_length].astype(jnp.bfloat16),
                value_gradient[lower : lower + shard_length].astype(jnp.bfloat16),
            ],
            axis=1,
        )
        returned = from_behind(part, -distance).astype(jnp.float32)
        key_sum = key_sum + returned[:, :kv_width]
        value_sum = value_sum + returned[:, kv_width:]
    key_out = key_sum.astype(jnp.bfloat16)
    value_out = value_sum.astype(jnp.bfloat16)

    feature_block = lax.all_to_all(layer_input[0], "cz", split_axis=1, concat_axis=0, tiled=True)
    value_group = lax.all_gather(value_out, "cz", axis=0, tiled=True)
    partial = lax.dot_general(
        feature_block,
        value_group,
        (((0,), (0,)), ((), ())),
        preferred_element_type=jnp.float32,
    )
    owners = lax.axis_size("cx") * lax.axis_size("dp")
    rows = partial.shape[0] // owners
    padded_rows = -(-rows // 8) * 8
    partial = partial.reshape(owners, rows, kv_width)
    partial = jnp.pad(partial, ((0, 0), (0, padded_rows - rows), (0, 0)))
    partial = partial.reshape(owners * padded_rows, kv_width)
    weight_grad = lax.psum_scatter(partial, ("cx", "dp"), scatter_dimension=0, tiled=True)
    weight_grad = weight_grad[:rows]

    square_total = jnp.sum(weight_grad * weight_grad)
    square_total = lax.psum(square_total, "dp")
    square_total = lax.psum(square_total, "cx")
    square_total = lax.psum(square_total, "cz")
    norm_total = jnp.sqrt(square_total + 1e-06)
    clipped = weight_grad * jnp.minimum(1.0, clip_norm / norm_total)
    new_first = beta_first * first_moment_value + (1.0 - beta_first) * clipped
    new_second = beta_second * second_moment_value + (1.0 - beta_second) * clipped * clipped
    step_dir = new_first / correct_first / (jnp.sqrt(new_second / correct_second) + adam_eps)
    new_master = master - learn_rate * (step_dir + decay_rate * master)
    new_weight = lax.all_gather(new_master.astype(jnp.bfloat16), "dp", axis=0, tiled=True)
    return (
        query_gradient[None],
        key_out[None],
        value_out[None],
        new_master,
        new_first,
        new_second,
        new_weight,
    )


def solution(mesh):
    n_ctx = mesh.shape["ctx"]
    n_dp = mesh.shape["dp"]
    z_size = Z_SIZE if n_ctx % Z_SIZE == 0 else n_ctx
    grid = Mesh(mesh.devices.reshape(z_size, n_ctx // z_size, n_dp), ("cz", "cx", "dp"))
    tokens = P("dp", CTX, None)
    owner = P(("cz", "cx", "dp"), None)
    return jax.shard_map(
        shards,
        mesh=grid,
        in_specs=(
            tokens,
            tokens,
            tokens,
            tokens,
            tokens,
            P("dp", CTX),
            owner,
            owner,
            owner,
        ),
        out_specs=(
            tokens,
            tokens,
            tokens,
            owner,
            owner,
            owner,
            P(CTX, None),
        ),
        check_vma=False,
    )
```

```python
import jax
import jax.numpy as jnp
from jax import lax
from jax.sharding import Mesh
from jax.sharding import PartitionSpec as P

QUERY_HEADS = 16
KEY_VALUE_HEADS = 8
HEAD_SIZE = 128
WINDOW = 1024
Z_SIZE = 8

CTX = ("cz", "cx")

query_scale = 168.0 ** (-0.5)
masked_score = -1e30
clip_norm = 1.0
beta_first = 0.9
beta_second = 0.95
learn_rate = 0.001
decay_rate = 0.1
adam_eps = 1e-08
correct_first = 0.9999734386011124
correct_second = 0.994079470779666


def ctx_size():
    return lax.axis_size("cz") * lax.axis_size("cx")


def ctx_index():
    return lax.axis_index("cz") * lax.axis_size("cx") + lax.axis_index("cx")


def from_behind(x, by):
    count = ctx_size()
    pairs = [(i, i + by) for i in range(count) if 0 <= i + by < count]
    return lax.ppermute(x, CTX, pairs)


def cyclic(x, axis, by):
    count = lax.axis_size(axis)
    return lax.ppermute(x, axis, [(i, (i + by) % count) for i in range(count)])


def attend(
    query_row_block,
    key_row_block,
    value_row_block,
    gradient_rows,
    seg_query,
    seg_key,
    index_query,
    index_key,
):
    shard_length = query_row_block.shape[0]
    extent_rows = key_row_block.shape[0]
    heads_ratio = QUERY_HEADS // KEY_VALUE_HEADS
    query_four_axes = query_row_block.reshape(shard_length, KEY_VALUE_HEADS, heads_ratio, HEAD_SIZE)
    gradient_four_axes = gradient_rows.reshape(
        shard_length, KEY_VALUE_HEADS, heads_ratio, HEAD_SIZE
    )
    key_three_axes = key_row_block.reshape(extent_rows, KEY_VALUE_HEADS, HEAD_SIZE)
    value_three_axes = value_row_block.reshape(extent_rows, KEY_VALUE_HEADS, HEAD_SIZE)
    scores = (
        jnp.einsum(
            "tgrd,egd->grte", query_four_axes, key_three_axes, preferred_element_type=jnp.float32
        )
        * query_scale
    )
    offset = index_query[:, None] - index_key[None, :]
    allowed = (
        (seg_query[:, None] == seg_key[None, :])
        & (offset >= 0)
        & (offset < WINDOW)
        & (index_key[None, :] >= 0)
    )
    scores = jnp.where(allowed, scores, masked_score)
    row_max = jnp.max(scores, axis=-1, keepdims=True)
    weights = jnp.exp(scores - row_max)
    probabilities = weights / jnp.sum(weights, axis=-1, keepdims=True)
    probs_low = probabilities.astype(jnp.bfloat16)
    attn_out = jnp.einsum(
        "grte,egd->tgrd", probs_low, value_three_axes, preferred_element_type=jnp.float32
    )
    row_delta = jnp.sum(gradient_four_axes.astype(jnp.float32) * attn_out, axis=-1)
    grad_probs = jnp.einsum(
        "tgrd,egd->grte", gradient_four_axes, value_three_axes, preferred_element_type=jnp.float32
    )
    grad_scores = probabilities * (grad_probs - jnp.transpose(row_delta, (1, 2, 0))[..., None])
    scores_low = grad_scores.astype(jnp.bfloat16)
    query_gradient = (
        jnp.einsum("grte,egd->tgrd", scores_low, key_three_axes, preferred_element_type=jnp.float32)
        * query_scale
    )
    query_gradient = query_gradient.astype(jnp.bfloat16).reshape(
        shard_length, QUERY_HEADS * HEAD_SIZE
    )
    key_gradient = (
        jnp.einsum(
            "grte,tgrd->egd", scores_low, query_four_axes, preferred_element_type=jnp.float32
        )
        * query_scale
    )
    value_gradient = jnp.einsum(
        "grte,tgrd->egd", probs_low, gradient_four_axes, preferred_element_type=jnp.float32
    )
    return (
        query_gradient,
        key_gradient.reshape(extent_rows, KEY_VALUE_HEADS * HEAD_SIZE),
        value_gradient.reshape(extent_rows, KEY_VALUE_HEADS * HEAD_SIZE),
    )


def shards(
    layer_input,
    query_states,
    key_states,
    value_state_rows,
    grad_out,
    segments,
    master,
    first_moment_value,
    second_moment_value,
):
    shard_length = query_states.shape[1]
    kv_width = key_states.shape[2]
    peer_count = min(WINDOW // shard_length, ctx_size() - 1)
    front_len = peer_count * shard_length
    position = ctx_index() * shard_length

    seg_query = segments[0]
    seg_cols = jnp.broadcast_to(seg_query.astype(jnp.bfloat16)[:, None], (shard_length, 128))
    own_kv = jnp.concatenate([key_states[0], value_state_rows[0], seg_cols], axis=1)
    incoming = [from_behind(own_kv, distance) for distance in range(peer_count, 0, -1)]
    kv_rows = jnp.concatenate(incoming + [own_kv], axis=0)
    key_row_block = kv_rows[:, :kv_width]
    value_row_block = kv_rows[:, kv_width : 2 * kv_width]
    seg_key = kv_rows[:, 2 * kv_width]
    index_query = position + jnp.arange(shard_length, dtype=jnp.int32)
    index_key = position - front_len + jnp.arange(front_len + shard_length, dtype=jnp.int32)
    query_gradient, key_gradient, value_gradient = attend(
        query_states[0],
        key_row_block,
        value_row_block,
        grad_out[0],
        seg_query.astype(jnp.bfloat16),
        seg_key,
        index_query,
        index_key,
    )
    key_sum = key_gradient[front_len:]
    value_sum = value_gradient[front_len:]
    for distance in range(1, peer_count + 1):
        lower = (peer_count - distance) * shard_length
        part = jnp.concatenate(
            [
                key_gradient[lower : lower + shard_length].astype(jnp.bfloat16),
                value_gradient[lower : lower + shard_length].astype(jnp.bfloat16),
            ],
            axis=1,
        )
        returned = from_behind(part, -distance).astype(jnp.float32)
        key_sum = key_sum + returned[:, :kv_width]
        value_sum = value_sum + returned[:, kv_width:]
    key_out = key_sum.astype(jnp.bfloat16)
    value_out = value_sum.astype(jnp.bfloat16)

    nz = lax.axis_size("cz")
    iz = lax.axis_index("cz")
    x_own = layer_input[0]
    width = x_own.shape[1] // nz
    x_list = [lax.dynamic_slice_in_dim(x_own, iz * width, width, 1)]
    v_list = [value_out]
    for shift in range(1, nz):
        target = (iz + shift) % nz
        piece = jnp.concatenate(
            [lax.dynamic_slice_in_dim(x_own, target * width, width, 1), value_out], axis=1
        )
        got = cyclic(piece, "cz", shift)
        x_list.append(got[:, :width])
        v_list.append(got[:, width:])
    partial = lax.dot_general(
        jnp.concatenate(x_list, axis=0),
        jnp.concatenate(v_list, axis=0),
        (((0,), (0,)), ((), ())),
        preferred_element_type=jnp.float32,
    )
    ncx = lax.axis_size("cx")
    ndp = lax.axis_size("dp")
    rows = width // (ncx * ndp)
    partial = partial.reshape(ncx, ndp, rows, kv_width)
    idp = lax.axis_index("dp")
    stage = lax.dynamic_index_in_dim(partial, idp, 1, keepdims=False)
    for shift in range(1, ndp):
        target = (idp + shift) % ndp
        stage = stage + cyclic(lax.dynamic_index_in_dim(partial, target, 1, keepdims=False), "dp", shift)
    icx = lax.axis_index("cx")
    weight_grad = lax.dynamic_index_in_dim(stage, icx, 0, keepdims=False)
    for shift in range(1, ncx):
        target = (icx + shift) % ncx
        weight_grad = weight_grad + cyclic(lax.dynamic_index_in_dim(stage, target, 0, keepdims=False), "cx", shift)

    square_total = jnp.sum(weight_grad * weight_grad)
    square_total = lax.psum(square_total, "dp")
    square_total = lax.psum(square_total, "cx")
    square_total = lax.psum(square_total, "cz")
    norm_total = jnp.sqrt(square_total + 1e-06)
    clipped = weight_grad * jnp.minimum(1.0, clip_norm / norm_total)
    new_first = beta_first * first_moment_value + (1.0 - beta_first) * clipped
    new_second = beta_second * second_moment_value + (1.0 - beta_second) * clipped * clipped
    step_dir = new_first / correct_first / (jnp.sqrt(new_second / correct_second) + adam_eps)
    new_master = master - learn_rate * (step_dir + decay_rate * master)
    new_weight = lax.all_gather(new_master.astype(jnp.bfloat16), "dp", axis=0, tiled=True)
    return (
        query_gradient[None],
        key_out[None],
        value_out[None],
        new_master,
        new_first,
        new_second,
        new_weight,
    )


def solution(mesh):
    n_ctx = mesh.shape["ctx"]
    n_dp = mesh.shape["dp"]
    z_size = Z_SIZE if n_ctx % Z_SIZE == 0 else n_ctx
    grid = Mesh(mesh.devices.reshape(z_size, n_ctx // z_size, n_dp), ("cz", "cx", "dp"))
    tokens = P("dp", CTX, None)
    owner = P(("cz", "cx", "dp"), None)
    return jax.shard_map(
        shards,
        mesh=grid,
        in_specs=(
            tokens,
            tokens,
            tokens,
            tokens,
            tokens,
            P("dp", CTX),
            owner,
            owner,
            owner,
        ),
        out_specs=(
            tokens,
            tokens,
            tokens,
            owner,
            owner,
            owner,
            P(CTX, None),
        ),
        check_vma=False,
    )
```

```python
import jax
import jax.numpy as jnp
from jax import lax
from jax.sharding import Mesh
from jax.sharding import PartitionSpec as P

QUERY_HEADS = 16
KEY_VALUE_HEADS = 8
HEAD_SIZE = 128
WINDOW = 1024
Z_SIZE = 8

CTX = ("cz", "cx")
DP = ("y", "core")

query_scale = 168.0 ** (-0.5)
masked_score = -1e30
clip_norm = 1.0
beta_first = 0.9
beta_second = 0.95
learn_rate = 0.001
decay_rate = 0.1
adam_eps = 1e-08
correct_first = 0.9999734386011124
correct_second = 0.994079470779666


def ctx_size():
    return lax.axis_size("cz") * lax.axis_size("cx")


def ctx_index():
    return lax.axis_index("cz") * lax.axis_size("cx") + lax.axis_index("cx")


def cyclic(x, axis, by):
    count = lax.axis_size(axis)
    return lax.ppermute(x, axis, [(i, (i + by) % count) for i in range(count)])


def attend(
    query_row_block,
    key_row_block,
    value_row_block,
    gradient_rows,
    seg_query,
    seg_key,
    index_query,
    index_key,
):
    shard_length = query_row_block.shape[0]
    extent_rows = key_row_block.shape[0]
    heads_ratio = QUERY_HEADS // KEY_VALUE_HEADS
    query_four_axes = query_row_block.reshape(shard_length, KEY_VALUE_HEADS, heads_ratio, HEAD_SIZE)
    gradient_four_axes = gradient_rows.reshape(
        shard_length, KEY_VALUE_HEADS, heads_ratio, HEAD_SIZE
    )
    key_three_axes = key_row_block.reshape(extent_rows, KEY_VALUE_HEADS, HEAD_SIZE)
    value_three_axes = value_row_block.reshape(extent_rows, KEY_VALUE_HEADS, HEAD_SIZE)
    scores = (
        jnp.einsum(
            "tgrd,egd->grte", query_four_axes, key_three_axes, preferred_element_type=jnp.float32
        )
        * query_scale
    )
    offset = index_query[:, None] - index_key[None, :]
    allowed = (
        (seg_query[:, None] == seg_key[None, :])
        & (offset >= 0)
        & (offset < WINDOW)
        & (index_key[None, :] >= 0)
    )
    scores = jnp.where(allowed, scores, masked_score)
    row_max = jnp.max(scores, axis=-1, keepdims=True)
    weights = jnp.exp(scores - row_max)
    probabilities = weights / jnp.sum(weights, axis=-1, keepdims=True)
    probs_low = probabilities.astype(jnp.bfloat16)
    attn_out = jnp.einsum(
        "grte,egd->tgrd", probs_low, value_three_axes, preferred_element_type=jnp.float32
    )
    row_delta = jnp.sum(gradient_four_axes.astype(jnp.float32) * attn_out, axis=-1)
    grad_probs = jnp.einsum(
        "tgrd,egd->grte", gradient_four_axes, value_three_axes, preferred_element_type=jnp.float32
    )
    grad_scores = probabilities * (grad_probs - jnp.transpose(row_delta, (1, 2, 0))[..., None])
    scores_low = grad_scores.astype(jnp.bfloat16)
    query_gradient = (
        jnp.einsum("grte,egd->tgrd", scores_low, key_three_axes, preferred_element_type=jnp.float32)
        * query_scale
    )
    query_gradient = query_gradient.astype(jnp.bfloat16).reshape(
        shard_length, QUERY_HEADS * HEAD_SIZE
    )
    key_gradient = (
        jnp.einsum(
            "grte,tgrd->egd", scores_low, query_four_axes, preferred_element_type=jnp.float32
        )
        * query_scale
    )
    value_gradient = jnp.einsum(
        "grte,tgrd->egd", probs_low, gradient_four_axes, preferred_element_type=jnp.float32
    )
    return (
        query_gradient,
        key_gradient.reshape(extent_rows, KEY_VALUE_HEADS * HEAD_SIZE),
        value_gradient.reshape(extent_rows, KEY_VALUE_HEADS * HEAD_SIZE),
    )


def shift(x, axis, by):
    count = lax.axis_size(axis)
    pairs = [(i, i + by) for i in range(count) if 0 <= i + by < count]
    return lax.ppermute(x, axis, pairs)


def all_sum(x, axes):
    for axis in axes:
        count = lax.axis_size(axis)
        step = 1
        while step < count:
            x = x + cyclic(x, axis, step)
            step *= 2
    return x


def shards(
    layer_input,
    query_states,
    key_states,
    value_state_rows,
    grad_out,
    segments,
    master,
    first_moment_value,
    second_moment_value,
):
    shard_length = query_states.shape[1]
    kv_width = key_states.shape[2]
    ncx = lax.axis_size("cx")
    icx = lax.axis_index("cx")
    iz = lax.axis_index("cz")
    assert WINDOW // shard_length == 2 * ncx
    block = ctx_index()

    seg_query = segments[0]
    seg_cols = jnp.broadcast_to(seg_query.astype(jnp.bfloat16)[:, None], (shard_length, 128))
    own_kv = jnp.concatenate([key_states[0], value_state_rows[0], seg_cols], axis=1)
    plane_one = shift(own_kv, "cz", 1)
    plane_two = shift(plane_one, "cz", 1)
    slots = [own_kv, plane_one, plane_two]
    sources = [block, block - ncx, block - 2 * ncx]
    wraps = []
    for by in range(1, ncx):
        slots.append(cyclic(plane_one, "cx", by))
        sources.append((iz - 1) * ncx + (icx - by) % ncx)
    for by in range(1, ncx):
        sending_wraps = icx + by >= ncx
        slots.append(cyclic(jnp.where(sending_wraps, plane_two, own_kv), "cx", by))
        got_wrap = icx - by < 0
        wraps.append(sending_wraps)
        sources.append(jnp.where(got_wrap, block - ncx - by, block - by))
    kv_rows = jnp.concatenate(slots, axis=0)
    key_row_block = kv_rows[:, :kv_width]
    value_row_block = kv_rows[:, kv_width : 2 * kv_width]
    seg_key = kv_rows[:, 2 * kv_width]
    index_query = block * shard_length + jnp.arange(shard_length, dtype=jnp.int32)
    index_key = jnp.concatenate(
        [src * shard_length + jnp.arange(shard_length, dtype=jnp.int32) for src in sources]
    )
    query_gradient, key_gradient, value_gradient = attend(
        query_states[0],
        key_row_block,
        value_row_block,
        grad_out[0],
        seg_query.astype(jnp.bfloat16),
        seg_key,
        index_query,
        index_key,
    )
    grads = jnp.concatenate([key_gradient, value_gradient], axis=1)
    slot_grads = [grads[i * shard_length : (i + 1) * shard_length] for i in range(len(slots))]
    low = lambda x: x.astype(jnp.bfloat16)
    own_acc = slot_grads[0]
    one_acc = low(slot_grads[1]).astype(jnp.float32)
    two_acc = low(slot_grads[2]).astype(jnp.float32)
    for k, by in enumerate(range(1, ncx)):
        back = cyclic(low(slot_grads[3 + k]), "cx", -by).astype(jnp.float32)
        one_acc = one_acc + back
    for k, by in enumerate(range(1, ncx)):
        back = cyclic(low(slot_grads[3 + (ncx - 1) + k]), "cx", -by).astype(jnp.float32)
        zero = jnp.zeros_like(back)
        two_acc = two_acc + jnp.where(wraps[k], back, zero)
        own_acc = own_acc + jnp.where(wraps[k], zero, back)
    one_acc = one_acc + shift(low(two_acc), "cz", -1).astype(jnp.float32)
    own_acc = own_acc + shift(low(one_acc), "cz", -1).astype(jnp.float32)
    key_out = own_acc[:, :kv_width].astype(jnp.bfloat16)
    value_out = own_acc[:, kv_width:].astype(jnp.bfloat16)

    nz = lax.axis_size("cz")
    ny = lax.axis_size("y")
    nc = lax.axis_size("core")
    x_own = layer_input[0]
    rows = x_own.shape[1] // (nz * ncx * ny * nc)
    x_view = x_own.reshape(shard_length, nz, ncx, ny * nc * rows)

    def columns(target):
        picked = lax.dynamic_index_in_dim(x_view, target, 2, keepdims=False)
        return picked.reshape(shard_length, nz * ny * nc * rows)

    x_list = [columns(icx)]
    v_list = [value_out]
    for by in range(1, ncx):
        piece = jnp.concatenate([columns((icx + by) % ncx), value_out], axis=1)
        got = cyclic(piece, "cx", by)
        x_list.append(got[:, : -kv_width])
        v_list.append(got[:, -kv_width:])
    partial = lax.dot_general(
        jnp.concatenate(x_list, axis=0),
        jnp.concatenate(v_list, axis=0),
        (((0,), (0,)), ((), ())),
        preferred_element_type=jnp.float32,
    )
    partial = partial.reshape(nz, ny, nc, rows, kv_width)
    icore = lax.axis_index("core")
    stage = lax.dynamic_index_in_dim(partial, icore, 2, keepdims=False)
    for by in range(1, nc):
        sent = lax.dynamic_index_in_dim(partial, (icore + by) % nc, 2, keepdims=False)
        stage = stage + cyclic(low(sent), "core", by).astype(jnp.float32)
    iy = lax.axis_index("y")
    stage_y = lax.dynamic_index_in_dim(stage, iy, 1, keepdims=False)
    for by in range(1, ny):
        sent = lax.dynamic_index_in_dim(stage, (iy + by) % ny, 1, keepdims=False)
        stage_y = stage_y + cyclic(low(sent), "y", by).astype(jnp.float32)
    weight_grad = lax.dynamic_index_in_dim(stage_y, iz, 0, keepdims=False)
    for by in range(1, nz):
        sent = lax.dynamic_index_in_dim(stage_y, (iz + by) % nz, 0, keepdims=False)
        weight_grad = weight_grad + cyclic(sent, "cz", by)

    square_total = all_sum(jnp.sum(weight_grad * weight_grad), ("core", "y", "cx", "cz"))
    norm_total = jnp.sqrt(square_total + 1e-06)
    clipped = weight_grad * jnp.minimum(1.0, clip_norm / norm_total)
    new_first = beta_first * first_moment_value + (1.0 - beta_first) * clipped
    new_second = beta_second * second_moment_value + (1.0 - beta_second) * clipped * clipped
    step_dir = new_first / correct_first / (jnp.sqrt(new_second / correct_second) + adam_eps)
    new_master = master - learn_rate * (step_dir + decay_rate * master)
    new_weight = lax.all_gather(new_master.astype(jnp.bfloat16), DP, axis=0, tiled=True)
    return (
        query_gradient[None],
        key_out[None],
        value_out[None],
        new_master,
        new_first,
        new_second,
        new_weight,
    )


def solution(mesh):
    n_ctx = mesh.shape["ctx"]
    n_dp = mesh.shape["dp"]
    z_size = Z_SIZE if n_ctx % Z_SIZE == 0 else n_ctx
    grid = Mesh(
        mesh.devices.reshape(z_size, n_ctx // z_size, n_dp // 2, 2), ("cz", "cx", "y", "core")
    )
    tokens = P(DP, CTX, None)
    owner = P(("cz", "cx", "y", "core"), None)
    return jax.shard_map(
        shards,
        mesh=grid,
        in_specs=(
            tokens,
            tokens,
            tokens,
            tokens,
            tokens,
            P(DP, CTX),
            owner,
            owner,
            owner,
        ),
        out_specs=(
            tokens,
            tokens,
            tokens,
            owner,
            owner,
            owner,
            P(CTX, None),
        ),
        check_vma=False,
    )
```

```python
import jax
import jax.numpy as jnp
from jax import lax
from jax.sharding import Mesh
from jax.sharding import PartitionSpec as P

QUERY_HEADS = 16
KEY_VALUE_HEADS = 8
HEAD_SIZE = 128
WINDOW = 1024
Z_SIZE = 8

CTX = ("cz", "cx")
DP = ("y", "core")

query_scale = 168.0 ** (-0.5)
masked_score = -1e30
clip_norm = 1.0
beta_first = 0.9
beta_second = 0.95
learn_rate = 0.001
decay_rate = 0.1
adam_eps = 1e-08
correct_first = 0.9999734386011124
correct_second = 0.994079470779666


def ctx_size():
    return lax.axis_size("cz") * lax.axis_size("cx")


def ctx_index():
    return lax.axis_index("cz") * lax.axis_size("cx") + lax.axis_index("cx")


def cyclic(x, axis, by):
    count = lax.axis_size(axis)
    return lax.ppermute(x, axis, [(i, (i + by) % count) for i in range(count)])


def attend(
    query_row_block,
    key_row_block,
    value_row_block,
    gradient_rows,
    seg_query,
    seg_key,
    index_query,
    index_key,
):
    shard_length = query_row_block.shape[0]
    extent_rows = key_row_block.shape[0]
    heads_ratio = QUERY_HEADS // KEY_VALUE_HEADS
    query_four_axes = query_row_block.reshape(shard_length, KEY_VALUE_HEADS, heads_ratio, HEAD_SIZE)
    gradient_four_axes = gradient_rows.reshape(
        shard_length, KEY_VALUE_HEADS, heads_ratio, HEAD_SIZE
    )
    key_three_axes = key_row_block.reshape(extent_rows, KEY_VALUE_HEADS, HEAD_SIZE)
    value_three_axes = value_row_block.reshape(extent_rows, KEY_VALUE_HEADS, HEAD_SIZE)
    scores = (
        jnp.einsum(
            "tgrd,egd->grte", query_four_axes, key_three_axes, preferred_element_type=jnp.float32
        )
        * query_scale
    )
    offset = index_query[:, None] - index_key[None, :]
    allowed = (
        (seg_query[:, None] == seg_key[None, :])
        & (offset >= 0)
        & (offset < WINDOW)
        & (index_key[None, :] >= 0)
    )
    scores = jnp.where(allowed, scores, masked_score)
    row_max = jnp.max(scores, axis=-1, keepdims=True)
    weights = jnp.exp(scores - row_max)
    probabilities = weights / jnp.sum(weights, axis=-1, keepdims=True)
    probs_low = probabilities.astype(jnp.bfloat16)
    attn_out = jnp.einsum(
        "grte,egd->tgrd", probs_low, value_three_axes, preferred_element_type=jnp.float32
    )
    row_delta = jnp.sum(gradient_four_axes.astype(jnp.float32) * attn_out, axis=-1)
    grad_probs = jnp.einsum(
        "tgrd,egd->grte", gradient_four_axes, value_three_axes, preferred_element_type=jnp.float32
    )
    grad_scores = probabilities * (grad_probs - jnp.transpose(row_delta, (1, 2, 0))[..., None])
    scores_low = grad_scores.astype(jnp.bfloat16)
    query_gradient = (
        jnp.einsum("grte,egd->tgrd", scores_low, key_three_axes, preferred_element_type=jnp.float32)
        * query_scale
    )
    query_gradient = query_gradient.astype(jnp.bfloat16).reshape(
        shard_length, QUERY_HEADS * HEAD_SIZE
    )
    key_gradient = (
        jnp.einsum(
            "grte,tgrd->egd", scores_low, query_four_axes, preferred_element_type=jnp.float32
        )
        * query_scale
    )
    value_gradient = jnp.einsum(
        "grte,tgrd->egd", probs_low, gradient_four_axes, preferred_element_type=jnp.float32
    )
    return (
        query_gradient,
        key_gradient.reshape(extent_rows, KEY_VALUE_HEADS * HEAD_SIZE),
        value_gradient.reshape(extent_rows, KEY_VALUE_HEADS * HEAD_SIZE),
    )


def shift(x, axis, by):
    count = lax.axis_size(axis)
    pairs = [(i, i + by) for i in range(count) if 0 <= i + by < count]
    return lax.ppermute(x, axis, pairs)


def all_sum(x, axes):
    for axis in axes:
        total = x
        for by in range(1, lax.axis_size(axis)):
            total = total + cyclic(x, axis, by)
        x = total
    return x


def halving_scatter(data, axis):
    count = lax.axis_size(axis)
    me = lax.axis_index(axis)
    distance = count // 2
    while distance >= 1:
        bit = (me // distance) % 2
        halves = data.reshape((2, data.shape[0] // 2) + data.shape[1:])
        keep = lax.dynamic_index_in_dim(halves, bit, 0, keepdims=False)
        sent = lax.dynamic_index_in_dim(halves, 1 - bit, 0, keepdims=False)
        pairs = [(i, i ^ distance) for i in range(count)]
        data = keep + lax.ppermute(sent, axis, pairs)
        distance //= 2
    return data[0]


def shards(
    layer_input,
    query_states,
    key_states,
    value_state_rows,
    grad_out,
    segments,
    master,
    first_moment_value,
    second_moment_value,
):
    shard_length = query_states.shape[1]
    kv_width = key_states.shape[2]
    ncx = lax.axis_size("cx")
    icx = lax.axis_index("cx")
    iz = lax.axis_index("cz")
    assert WINDOW // shard_length == 2 * ncx
    block = ctx_index()

    seg_query = segments[0]
    seg_cols = jnp.broadcast_to(seg_query.astype(jnp.bfloat16)[:, None], (shard_length, 128))
    own_kv = jnp.concatenate([key_states[0], value_state_rows[0], seg_cols], axis=1)
    plane_one = shift(own_kv, "cz", 1)
    plane_two = shift(plane_one, "cz", 1)
    slots = [own_kv, plane_one, plane_two]
    sources = [block, block - ncx, block - 2 * ncx]
    wraps = []
    for by in range(1, ncx):
        slots.append(cyclic(plane_one, "cx", by))
        sources.append((iz - 1) * ncx + (icx - by) % ncx)
    for by in range(1, ncx):
        sending_wraps = icx + by >= ncx
        slots.append(cyclic(jnp.where(sending_wraps, plane_two, own_kv), "cx", by))
        got_wrap = icx - by < 0
        wraps.append(sending_wraps)
        sources.append(jnp.where(got_wrap, block - ncx - by, block - by))
    kv_rows = jnp.concatenate(slots, axis=0)
    key_row_block = kv_rows[:, :kv_width]
    value_row_block = kv_rows[:, kv_width : 2 * kv_width]
    seg_key = kv_rows[:, 2 * kv_width]
    index_query = block * shard_length + jnp.arange(shard_length, dtype=jnp.int32)
    index_key = jnp.concatenate(
        [src * shard_length + jnp.arange(shard_length, dtype=jnp.int32) for src in sources]
    )
    query_gradient, key_gradient, value_gradient = attend(
        query_states[0],
        key_row_block,
        value_row_block,
        grad_out[0],
        seg_query.astype(jnp.bfloat16),
        seg_key,
        index_query,
        index_key,
    )
    grads = jnp.concatenate([key_gradient, value_gradient], axis=1)
    slot_grads = [grads[i * shard_length : (i + 1) * shard_length] for i in range(len(slots))]
    low = lambda x: x.astype(jnp.bfloat16)
    own_acc = slot_grads[0]
    one_acc = low(slot_grads[1]).astype(jnp.float32)
    two_acc = low(slot_grads[2]).astype(jnp.float32)
    for k, by in enumerate(range(1, ncx)):
        back = cyclic(low(slot_grads[3 + k]), "cx", -by).astype(jnp.float32)
        one_acc = one_acc + back
    for k, by in enumerate(range(1, ncx)):
        back = cyclic(low(slot_grads[3 + (ncx - 1) + k]), "cx", -by).astype(jnp.float32)
        zero = jnp.zeros_like(back)
        two_acc = two_acc + jnp.where(wraps[k], back, zero)
        own_acc = own_acc + jnp.where(wraps[k], zero, back)
    one_acc = one_acc + shift(low(two_acc), "cz", -1).astype(jnp.float32)
    own_acc = own_acc + shift(low(one_acc), "cz", -1).astype(jnp.float32)
    key_out = own_acc[:, :kv_width].astype(jnp.bfloat16)
    value_out = own_acc[:, kv_width:].astype(jnp.bfloat16)

    nz = lax.axis_size("cz")
    ny = lax.axis_size("y")
    nc = lax.axis_size("core")
    x_own = layer_input[0]
    rows = x_own.shape[1] // (nz * ncx * ny * nc)
    x_view = x_own.reshape(shard_length, nz, ncx, ny * nc * rows)

    def columns(target):
        picked = lax.dynamic_index_in_dim(x_view, target, 2, keepdims=False)
        return picked.reshape(shard_length, nz * ny * nc * rows)

    x_list = [columns(icx)]
    v_list = [value_out]
    x_late, _ = lax.optimization_barrier((x_view, kv_rows))
    x_view = x_late
    for by in range(1, ncx):
        x_list.append(cyclic(columns((icx + by) % ncx), "cx", by))
        v_list.append(cyclic(value_out, "cx", by))
    partial = lax.dot_general(
        jnp.concatenate(x_list, axis=0),
        jnp.concatenate(v_list, axis=0),
        (((0,), (0,)), ((), ())),
        preferred_element_type=jnp.float32,
    )
    partial = partial.reshape(nz, ny, nc, rows, kv_width)
    icore = lax.axis_index("core")
    stage = lax.dynamic_index_in_dim(partial, icore, 2, keepdims=False)
    for by in range(1, nc):
        sent = lax.dynamic_index_in_dim(partial, (icore + by) % nc, 2, keepdims=False)
        stage = stage + cyclic(low(sent), "core", by).astype(jnp.float32)
    iy = lax.axis_index("y")
    stage_y = lax.dynamic_index_in_dim(stage, iy, 1, keepdims=False)
    for by in range(1, ny):
        sent = lax.dynamic_index_in_dim(stage, (iy + by) % ny, 1, keepdims=False)
        stage_y = stage_y + cyclic(low(sent), "y", by).astype(jnp.float32)
    weight_grad = halving_scatter(stage_y, "cz")

    square_total = all_sum(jnp.sum(weight_grad * weight_grad), ("core", "y", "cx", "cz"))
    norm_total = jnp.sqrt(square_total + 1e-06)
    clipped = weight_grad * jnp.minimum(1.0, clip_norm / norm_total)
    new_first = beta_first * first_moment_value + (1.0 - beta_first) * clipped
    new_second = beta_second * second_moment_value + (1.0 - beta_second) * clipped * clipped
    step_dir = new_first / correct_first / (jnp.sqrt(new_second / correct_second) + adam_eps)
    new_master = master - learn_rate * (step_dir + decay_rate * master)
    new_weight = lax.all_gather(new_master.astype(jnp.bfloat16), DP, axis=0, tiled=True)
    return (
        query_gradient[None],
        key_out[None],
        value_out[None],
        new_master,
        new_first,
        new_second,
        new_weight,
    )


def solution(mesh):
    n_ctx = mesh.shape["ctx"]
    n_dp = mesh.shape["dp"]
    z_size = Z_SIZE if n_ctx % Z_SIZE == 0 else n_ctx
    grid = Mesh(
        mesh.devices.reshape(z_size, n_ctx // z_size, n_dp // 2, 2), ("cz", "cx", "y", "core")
    )
    tokens = P(DP, CTX, None)
    owner = P(("cz", "cx", "y", "core"), None)
    return jax.shard_map(
        shards,
        mesh=grid,
        in_specs=(
            tokens,
            tokens,
            tokens,
            tokens,
            tokens,
            P(DP, CTX),
            owner,
            owner,
            owner,
        ),
        out_specs=(
            tokens,
            tokens,
            tokens,
            owner,
            owner,
            owner,
            P(CTX, None),
        ),
        check_vma=False,
    )
```

```python
import math

import jax
import jax.numpy as jnp
from jax import lax
from jax.sharding import Mesh
from jax.sharding import PartitionSpec as P

QUERY_HEADS = 16
KEY_VALUE_HEADS = 8
HEAD_SIZE = 128
WINDOW = 1024
Z_SIZE = 8

CTX = ("cz", "cx")
DP = ("y", "core")

query_scale = 168.0 ** (-0.5)
masked_score = -1e30
clip_norm = 1.0
beta_first = 0.9
beta_second = 0.95
learn_rate = 0.001
decay_rate = 0.1
adam_eps = 1e-08
correct_first = 0.9999734386011124
correct_second = 0.994079470779666


def ctx_size():
    return lax.axis_size("cz") * lax.axis_size("cx")


def ctx_index():
    return lax.axis_index("cz") * lax.axis_size("cx") + lax.axis_index("cx")


def cyclic(x, axis, by):
    count = lax.axis_size(axis) if isinstance(axis, str) else math.prod(lax.axis_size(a) for a in axis)
    return lax.ppermute(x, axis, [(i, (i + by) % count) for i in range(count)])


def attend(
    query_row_block,
    key_row_block,
    value_row_block,
    gradient_rows,
    seg_query,
    seg_key,
    index_query,
    index_key,
):
    shard_length = query_row_block.shape[0]
    extent_rows = key_row_block.shape[0]
    heads_ratio = QUERY_HEADS // KEY_VALUE_HEADS
    query_four_axes = query_row_block.reshape(shard_length, KEY_VALUE_HEADS, heads_ratio, HEAD_SIZE)
    gradient_four_axes = gradient_rows.reshape(
        shard_length, KEY_VALUE_HEADS, heads_ratio, HEAD_SIZE
    )
    key_three_axes = key_row_block.reshape(extent_rows, KEY_VALUE_HEADS, HEAD_SIZE)
    value_three_axes = value_row_block.reshape(extent_rows, KEY_VALUE_HEADS, HEAD_SIZE)
    scores = (
        jnp.einsum(
            "tgrd,egd->grte", query_four_axes, key_three_axes, preferred_element_type=jnp.float32
        )
        * query_scale
    )
    offset = index_query[:, None] - index_key[None, :]
    allowed = (
        (seg_query[:, None] == seg_key[None, :])
        & (offset >= 0)
        & (offset < WINDOW)
        & (index_key[None, :] >= 0)
    )
    scores = jnp.where(allowed, scores, masked_score)
    row_max = jnp.max(scores, axis=-1, keepdims=True)
    weights = jnp.exp(scores - row_max)
    probabilities = weights / jnp.sum(weights, axis=-1, keepdims=True)
    probs_low = probabilities.astype(jnp.bfloat16)
    attn_out = jnp.einsum(
        "grte,egd->tgrd", probs_low, value_three_axes, preferred_element_type=jnp.float32
    )
    row_delta = jnp.sum(gradient_four_axes.astype(jnp.float32) * attn_out, axis=-1)
    grad_probs = jnp.einsum(
        "tgrd,egd->grte", gradient_four_axes, value_three_axes, preferred_element_type=jnp.float32
    )
    grad_scores = probabilities * (grad_probs - jnp.transpose(row_delta, (1, 2, 0))[..., None])
    scores_low = grad_scores.astype(jnp.bfloat16)
    query_gradient = (
        jnp.einsum("grte,egd->tgrd", scores_low, key_three_axes, preferred_element_type=jnp.float32)
        * query_scale
    )
    query_gradient = query_gradient.astype(jnp.bfloat16).reshape(
        shard_length, QUERY_HEADS * HEAD_SIZE
    )
    key_gradient = (
        jnp.einsum(
            "grte,tgrd->egd", scores_low, query_four_axes, preferred_element_type=jnp.float32
        )
        * query_scale
    )
    value_gradient = jnp.einsum(
        "grte,tgrd->egd", probs_low, gradient_four_axes, preferred_element_type=jnp.float32
    )
    return (
        query_gradient,
        key_gradient.reshape(extent_rows, KEY_VALUE_HEADS * HEAD_SIZE),
        value_gradient.reshape(extent_rows, KEY_VALUE_HEADS * HEAD_SIZE),
    )


def shift(x, axis, by):
    count = lax.axis_size(axis)
    pairs = [(i, i + by) for i in range(count) if 0 <= i + by < count]
    return lax.ppermute(x, axis, pairs)


def wrapped(x, axis, by, back=False):
    count = lax.axis_size(axis)
    pairs = [(i, i + by - count) for i in range(count) if i + by >= count]
    if back:
        pairs = [(b, a) for a, b in pairs]
    return lax.ppermute(x, axis, pairs)


def all_sum(x, axes):
    for axis in axes:
        count = lax.axis_size(axis)
        step = 1
        while step < count:
            x = x + cyclic(x, axis, step)
            step *= 2
    return x


def shards(
    layer_input,
    query_states,
    key_states,
    value_state_rows,
    grad_out,
    segments,
    master,
    first_moment_value,
    second_moment_value,
):
    shard_length = query_states.shape[1]
    kv_width = key_states.shape[2]
    ncx = lax.axis_size("cx")
    icx = lax.axis_index("cx")
    iz = lax.axis_index("cz")
    assert WINDOW // shard_length == 2 * ncx
    block = ctx_index()

    seg_query = segments[0]
    seg_cols = jnp.broadcast_to(seg_query.astype(jnp.bfloat16)[:, None], (shard_length, 128))
    own_kv = jnp.concatenate([key_states[0], value_state_rows[0], seg_cols], axis=1)
    plane_one = shift(own_kv, "cz", 1)
    plane_two = shift(plane_one, "cz", 1)
    slots = [own_kv, plane_one, plane_two]
    sources = [block, block - ncx, block - 2 * ncx]
    wraps = []
    for by in range(1, ncx):
        slots.append(cyclic(plane_one, "cx", by))
        sources.append((iz - 1) * ncx + (icx - by) % ncx)
    for by in range(1, ncx):
        got_wrap = icx - by < 0
        plain = shift(own_kv, "cx", by)
        far = wrapped(plane_two, "cx", by)
        slots.append(jnp.where(got_wrap, far, plain))
        sources.append(jnp.where(got_wrap, block - ncx - by, block - by))
    kv_rows = jnp.concatenate(slots, axis=0)
    key_row_block = kv_rows[:, :kv_width]
    value_row_block = kv_rows[:, kv_width : 2 * kv_width]
    seg_key = kv_rows[:, 2 * kv_width]
    index_query = block * shard_length + jnp.arange(shard_length, dtype=jnp.int32)
    index_key = jnp.concatenate(
        [src * shard_length + jnp.arange(shard_length, dtype=jnp.int32) for src in sources]
    )
    query_gradient, key_gradient, value_gradient = attend(
        query_states[0],
        key_row_block,
        value_row_block,
        grad_out[0],
        seg_query.astype(jnp.bfloat16),
        seg_key,
        index_query,
        index_key,
    )
    grads = jnp.concatenate([key_gradient, value_gradient], axis=1)
    slot_grads = [grads[i * shard_length : (i + 1) * shard_length] for i in range(len(slots))]
    low = lambda x: x.astype(jnp.bfloat16)
    own_acc = slot_grads[0]
    one_acc = low(slot_grads[1]).astype(jnp.float32)
    two_acc = low(slot_grads[2]).astype(jnp.float32)
    for k, by in enumerate(range(1, ncx)):
        back = cyclic(low(slot_grads[3 + k]), "cx", -by).astype(jnp.float32)
        one_acc = one_acc + back
    for k, by in enumerate(range(1, ncx)):
        sent = low(slot_grads[3 + (ncx - 1) + k])
        own_acc = own_acc + shift(sent, "cx", -by).astype(jnp.float32)
        two_acc = two_acc + wrapped(sent, "cx", by, back=True).astype(jnp.float32)
    one_acc = one_acc + shift(low(two_acc), "cz", -1).astype(jnp.float32)
    own_acc = own_acc + shift(low(one_acc), "cz", -1).astype(jnp.float32)
    key_out = own_acc[:, :kv_width].astype(jnp.bfloat16)
    value_out = own_acc[:, kv_width:].astype(jnp.bfloat16)

    nz = lax.axis_size("cz")
    ndp = lax.axis_size("y") * lax.axis_size("core")
    idp = lax.axis_index("y") * lax.axis_size("core") + lax.axis_index("core")
    x_own = layer_input[0]
    rows = x_own.shape[1] // (nz * ncx * ndp)
    x_view = x_own.reshape(shard_length, nz * ncx, ndp, rows)

    def columns(target):
        picked = lax.dynamic_index_in_dim(x_view, target, 2, keepdims=False)
        return picked.reshape(shard_length, nz * ncx * rows)

    x_list = [columns(idp)]
    v_list = [value_out]
    for by in range(1, ndp):
        x_list.append(cyclic(columns((idp + by) % ndp), DP, by))
        v_list.append(cyclic(value_out, DP, by))
    partial = lax.dot_general(
        jnp.concatenate(x_list, axis=0),
        jnp.concatenate(v_list, axis=0),
        (((0,), (0,)), ((), ())),
        preferred_element_type=jnp.float32,
    )
    partial = partial.reshape(nz, ncx, rows, kv_width)
    stage = lax.dynamic_index_in_dim(partial, icx, 1, keepdims=False)
    for by in range(1, ncx):
        sent = lax.dynamic_index_in_dim(partial, (icx + by) % ncx, 1, keepdims=False)
        stage = stage + cyclic(low(sent), "cx", by).astype(jnp.float32)
    weight_grad = lax.dynamic_index_in_dim(stage, iz, 0, keepdims=False)
    for by in range(1, nz):
        sent = lax.dynamic_index_in_dim(stage, (iz + by) % nz, 0, keepdims=False)
        weight_grad = weight_grad + cyclic(sent, "cz", by)

    square_total = all_sum(jnp.sum(weight_grad * weight_grad), ("core", "y", "cx", "cz"))
    norm_total = jnp.sqrt(square_total + 1e-06)
    clipped = weight_grad * jnp.minimum(1.0, clip_norm / norm_total)
    new_first = beta_first * first_moment_value + (1.0 - beta_first) * clipped
    new_second = beta_second * second_moment_value + (1.0 - beta_second) * clipped * clipped
    step_dir = new_first / correct_first / (jnp.sqrt(new_second / correct_second) + adam_eps)
    new_master = master - learn_rate * (step_dir + decay_rate * master)
    new_weight = lax.all_gather(new_master.astype(jnp.bfloat16), DP, axis=0, tiled=True)
    return (
        query_gradient[None],
        key_out[None],
        value_out[None],
        new_master,
        new_first,
        new_second,
        new_weight,
    )


def solution(mesh):
    n_ctx = mesh.shape["ctx"]
    n_dp = mesh.shape["dp"]
    z_size = Z_SIZE if n_ctx % Z_SIZE == 0 else n_ctx
    grid = Mesh(
        mesh.devices.reshape(z_size, n_ctx // z_size, n_dp // 2, 2), ("cz", "cx", "y", "core")
    )
    tokens = P(DP, CTX, None)
    owner = P(("cz", "cx", "y", "core"), None)
    return jax.shard_map(
        shards,
        mesh=grid,
        in_specs=(
            tokens,
            tokens,
            tokens,
            tokens,
            tokens,
            P(DP, CTX),
            owner,
            owner,
            owner,
        ),
        out_specs=(
            tokens,
            tokens,
            tokens,
            owner,
            owner,
            owner,
            P(CTX, None),
        ),
        check_vma=False,
    )
```

```python
import jax
import jax.numpy as jnp
from jax import lax
from jax.sharding import Mesh
from jax.sharding import PartitionSpec as P

QUERY_HEADS = 16
KEY_VALUE_HEADS = 8
HEAD_SIZE = 128
WINDOW = 1024
Z_SIZE = 8

CTX = ("cz", "cx")
DP = ("y", "core")

query_scale = 168.0 ** (-0.5)
masked_score = -1e30
clip_norm = 1.0
beta_first = 0.9
beta_second = 0.95
learn_rate = 0.001
decay_rate = 0.1
adam_eps = 1e-08
correct_first = 0.9999734386011124
correct_second = 0.994079470779666


def ctx_size():
    return lax.axis_size("cz") * lax.axis_size("cx")


def ctx_index():
    return lax.axis_index("cz") * lax.axis_size("cx") + lax.axis_index("cx")


def cyclic(x, axis, by):
    count = lax.axis_size(axis)
    return lax.ppermute(x, axis, [(i, (i + by) % count) for i in range(count)])


def attend(
    query_row_block,
    key_row_block,
    value_row_block,
    gradient_rows,
    seg_query,
    seg_key,
    index_query,
    index_key,
):
    shard_length = query_row_block.shape[0]
    extent_rows = key_row_block.shape[0]
    heads_ratio = QUERY_HEADS // KEY_VALUE_HEADS
    query_four_axes = query_row_block.reshape(shard_length, KEY_VALUE_HEADS, heads_ratio, HEAD_SIZE)
    gradient_four_axes = gradient_rows.reshape(
        shard_length, KEY_VALUE_HEADS, heads_ratio, HEAD_SIZE
    )
    key_three_axes = key_row_block.reshape(extent_rows, KEY_VALUE_HEADS, HEAD_SIZE)
    value_three_axes = value_row_block.reshape(extent_rows, KEY_VALUE_HEADS, HEAD_SIZE)
    scores = (
        jnp.einsum(
            "tgrd,egd->grte", query_four_axes, key_three_axes, preferred_element_type=jnp.float32
        )
        * query_scale
    )
    offset = index_query[:, None] - index_key[None, :]
    allowed = (
        (seg_query[:, None] == seg_key[None, :])
        & (offset >= 0)
        & (offset < WINDOW)
        & (index_key[None, :] >= 0)
    )
    scores = jnp.where(allowed, scores, masked_score)
    row_max = jnp.max(scores, axis=-1, keepdims=True)
    weights = jnp.exp(scores - row_max)
    probabilities = weights / jnp.sum(weights, axis=-1, keepdims=True)
    probs_low = probabilities.astype(jnp.bfloat16)
    attn_out = jnp.einsum(
        "grte,egd->tgrd", probs_low, value_three_axes, preferred_element_type=jnp.float32
    )
    row_delta = jnp.sum(gradient_four_axes.astype(jnp.float32) * attn_out, axis=-1)
    grad_probs = jnp.einsum(
        "tgrd,egd->grte", gradient_four_axes, value_three_axes, preferred_element_type=jnp.float32
    )
    grad_scores = probabilities * (grad_probs - jnp.transpose(row_delta, (1, 2, 0))[..., None])
    scores_low = grad_scores.astype(jnp.bfloat16)
    query_gradient = (
        jnp.einsum("grte,egd->tgrd", scores_low, key_three_axes, preferred_element_type=jnp.float32)
        * query_scale
    )
    query_gradient = query_gradient.astype(jnp.bfloat16).reshape(
        shard_length, QUERY_HEADS * HEAD_SIZE
    )
    key_gradient = (
        jnp.einsum(
            "grte,tgrd->egd", scores_low, query_four_axes, preferred_element_type=jnp.float32
        )
        * query_scale
    )
    value_gradient = jnp.einsum(
        "grte,tgrd->egd", probs_low, gradient_four_axes, preferred_element_type=jnp.float32
    )
    return (
        query_gradient,
        key_gradient.reshape(extent_rows, KEY_VALUE_HEADS * HEAD_SIZE),
        value_gradient.reshape(extent_rows, KEY_VALUE_HEADS * HEAD_SIZE),
    )


def shift(x, axis, by):
    count = lax.axis_size(axis)
    pairs = [(i, i + by) for i in range(count) if 0 <= i + by < count]
    return lax.ppermute(x, axis, pairs)


def all_sum(x, axes):
    for axis in axes:
        count = lax.axis_size(axis)
        step = 1
        while step < count:
            x = x + cyclic(x, axis, step)
            step *= 2
    return x


def shards(
    layer_input,
    query_states,
    key_states,
    value_state_rows,
    grad_out,
    segments,
    master,
    first_moment_value,
    second_moment_value,
):
    shard_length = query_states.shape[1]
    kv_width = key_states.shape[2]
    ncx = lax.axis_size("cx")
    icx = lax.axis_index("cx")
    iz = lax.axis_index("cz")
    assert WINDOW // shard_length == 2 * ncx
    block = ctx_index()

    seg_query = segments[0]
    seg_cols = jnp.broadcast_to(seg_query.astype(jnp.bfloat16)[:, None], (shard_length, 128))
    own_kv = jnp.concatenate([key_states[0], value_state_rows[0], seg_cols], axis=1)
    plane_one = shift(own_kv, "cz", 1)
    plane_two = shift(plane_one, "cz", 1)
    slots = [own_kv, plane_one, plane_two]
    sources = [block, block - ncx, block - 2 * ncx]
    wraps = []
    for by in range(1, ncx):
        slots.append(cyclic(plane_one, "cx", by))
        sources.append((iz - 1) * ncx + (icx - by) % ncx)
    for by in range(1, ncx):
        sending_wraps = icx + by >= ncx
        slots.append(cyclic(jnp.where(sending_wraps, plane_two, own_kv), "cx", by))
        got_wrap = icx - by < 0
        wraps.append(sending_wraps)
        sources.append(jnp.where(got_wrap, block - ncx - by, block - by))
    kv_rows = jnp.concatenate(slots, axis=0)
    key_row_block = kv_rows[:, :kv_width]
    value_row_block = kv_rows[:, kv_width : 2 * kv_width]
    seg_key = kv_rows[:, 2 * kv_width]
    index_query = block * shard_length + jnp.arange(shard_length, dtype=jnp.int32)
    index_key = jnp.concatenate(
        [src * shard_length + jnp.arange(shard_length, dtype=jnp.int32) for src in sources]
    )
    query_gradient, key_gradient, value_gradient = attend(
        query_states[0],
        key_row_block,
        value_row_block,
        grad_out[0],
        seg_query.astype(jnp.bfloat16),
        seg_key,
        index_query,
        index_key,
    )
    grads = jnp.concatenate([key_gradient, value_gradient], axis=1)
    slot_grads = [grads[i * shard_length : (i + 1) * shard_length] for i in range(len(slots))]
    low = lambda x: x.astype(jnp.bfloat16)
    own_acc = slot_grads[0]
    one_acc = low(slot_grads[1]).astype(jnp.float32)
    two_acc = low(slot_grads[2]).astype(jnp.float32)
    for k, by in enumerate(range(1, ncx)):
        back = cyclic(low(slot_grads[3 + k]), "cx", -by).astype(jnp.float32)
        one_acc = one_acc + back
    for k, by in enumerate(range(1, ncx)):
        back = cyclic(low(slot_grads[3 + (ncx - 1) + k]), "cx", -by).astype(jnp.float32)
        zero = jnp.zeros_like(back)
        two_acc = two_acc + jnp.where(wraps[k], back, zero)
        own_acc = own_acc + jnp.where(wraps[k], zero, back)
    one_acc = one_acc + shift(low(two_acc), "cz", -1).astype(jnp.float32)
    own_acc = own_acc + shift(low(one_acc), "cz", -1).astype(jnp.float32)
    key_out = own_acc[:, :kv_width].astype(jnp.bfloat16)
    value_out = own_acc[:, kv_width:].astype(jnp.bfloat16)

    nz = lax.axis_size("cz")
    ny = lax.axis_size("y")
    nc = lax.axis_size("core")
    x_own = layer_input[0]
    rows = x_own.shape[1] // (nz * ncx * ny * nc)
    tall = -(-rows // 8) * 8
    x_view = x_own.reshape(shard_length, nz, ncx, ny * nc, rows)
    x_view = jnp.pad(x_view, ((0, 0), (0, 0), (0, 0), (0, 0), (0, tall - rows)))

    def columns(target):
        picked = lax.dynamic_index_in_dim(x_view, target, 2, keepdims=False)
        return picked.reshape(shard_length, nz * ny * nc * tall)

    x_list = [columns(icx)]
    v_list = [value_out]
    for by in range(1, ncx):
        piece = jnp.concatenate([columns((icx + by) % ncx), value_out], axis=1)
        got = cyclic(piece, "cx", by)
        x_list.append(got[:, : -kv_width])
        v_list.append(got[:, -kv_width:])
    partial = lax.dot_general(
        jnp.concatenate(x_list, axis=0),
        jnp.concatenate(v_list, axis=0),
        (((0,), (0,)), ((), ())),
        preferred_element_type=jnp.float32,
    )
    partial = partial.reshape(nz, ny, nc, tall, kv_width)
    icore = lax.axis_index("core")
    stage = lax.dynamic_index_in_dim(partial, icore, 2, keepdims=False)
    for by in range(1, nc):
        sent = lax.dynamic_index_in_dim(partial, (icore + by) % nc, 2, keepdims=False)
        stage = stage + cyclic(low(sent), "core", by).astype(jnp.float32)
    iy = lax.axis_index("y")
    stage_y = lax.dynamic_index_in_dim(stage, iy, 1, keepdims=False)
    for by in range(1, ny):
        sent = lax.dynamic_index_in_dim(stage, (iy + by) % ny, 1, keepdims=False)
        stage_y = stage_y + cyclic(low(sent), "y", by).astype(jnp.float32)
    weight_grad = lax.dynamic_index_in_dim(stage_y, iz, 0, keepdims=False)
    for by in range(1, nz):
        sent = lax.dynamic_index_in_dim(stage_y, (iz + by) % nz, 0, keepdims=False)
        weight_grad = weight_grad + cyclic(sent, "cz", by)

    weight_grad = weight_grad[:rows]
    square_total = lax.psum(jnp.sum(weight_grad * weight_grad), DP)
    square_total = all_sum(square_total, ("cx", "cz"))
    norm_total = jnp.sqrt(square_total + 1e-06)
    clipped = weight_grad * jnp.minimum(1.0, clip_norm / norm_total)
    new_first = beta_first * first_moment_value + (1.0 - beta_first) * clipped
    new_second = beta_second * second_moment_value + (1.0 - beta_second) * clipped * clipped
    step_dir = new_first / correct_first / (jnp.sqrt(new_second / correct_second) + adam_eps)
    new_master = master - learn_rate * (step_dir + decay_rate * master)
    new_weight = lax.all_gather(new_master.astype(jnp.bfloat16), DP, axis=0, tiled=True)
    return (
        query_gradient[None],
        key_out[None],
        value_out[None],
        new_master,
        new_first,
        new_second,
        new_weight,
    )


def solution(mesh):
    n_ctx = mesh.shape["ctx"]
    n_dp = mesh.shape["dp"]
    z_size = Z_SIZE if n_ctx % Z_SIZE == 0 else n_ctx
    grid = Mesh(
        mesh.devices.reshape(z_size, n_ctx // z_size, n_dp // 2, 2), ("cz", "cx", "y", "core")
    )
    tokens = P(DP, CTX, None)
    owner = P(("cz", "cx", "y", "core"), None)
    return jax.shard_map(
        shards,
        mesh=grid,
        in_specs=(
            tokens,
            tokens,
            tokens,
            tokens,
            tokens,
            P(DP, CTX),
            owner,
            owner,
            owner,
        ),
        out_specs=(
            tokens,
            tokens,
            tokens,
            owner,
            owner,
            owner,
            P(CTX, None),
        ),
        check_vma=False,
    )
```

```python
import jax
import jax.numpy as jnp
from jax import lax
from jax.sharding import Mesh
from jax.sharding import PartitionSpec as P

QUERY_HEADS = 16
KEY_VALUE_HEADS = 8
HEAD_SIZE = 128
WINDOW = 1024
Z_SIZE = 8

CTX = ("cz", "cx")
DP = ("y", "core")

query_scale = 168.0 ** (-0.5)
masked_score = -1e30
clip_norm = 1.0
beta_first = 0.9
beta_second = 0.95
learn_rate = 0.001
decay_rate = 0.1
adam_eps = 1e-08
correct_first = 0.9999734386011124
correct_second = 0.994079470779666


def ctx_size():
    return lax.axis_size("cz") * lax.axis_size("cx")


def ctx_index():
    return lax.axis_index("cz") * lax.axis_size("cx") + lax.axis_index("cx")


def cyclic(x, axis, by):
    count = lax.axis_size(axis)
    return lax.ppermute(x, axis, [(i, (i + by) % count) for i in range(count)])


def attend(
    query_row_block,
    key_row_block,
    value_row_block,
    gradient_rows,
    seg_query,
    seg_key,
    index_query,
    index_key,
):
    shard_length = query_row_block.shape[0]
    extent_rows = key_row_block.shape[0]
    heads_ratio = QUERY_HEADS // KEY_VALUE_HEADS
    query_four_axes = query_row_block.reshape(shard_length, KEY_VALUE_HEADS, heads_ratio, HEAD_SIZE)
    gradient_four_axes = gradient_rows.reshape(
        shard_length, KEY_VALUE_HEADS, heads_ratio, HEAD_SIZE
    )
    key_three_axes = key_row_block.reshape(extent_rows, KEY_VALUE_HEADS, HEAD_SIZE)
    value_three_axes = value_row_block.reshape(extent_rows, KEY_VALUE_HEADS, HEAD_SIZE)
    scores = (
        jnp.einsum(
            "tgrd,egd->grte", query_four_axes, key_three_axes, preferred_element_type=jnp.float32
        )
        * query_scale
    )
    offset = index_query[:, None] - index_key[None, :]
    allowed = (
        (seg_query[:, None] == seg_key[None, :])
        & (offset >= 0)
        & (offset < WINDOW)
        & (index_key[None, :] >= 0)
    )
    scores = jnp.where(allowed, scores, masked_score)
    row_max = jnp.max(scores, axis=-1, keepdims=True)
    weights = jnp.exp(scores - row_max)
    probabilities = weights / jnp.sum(weights, axis=-1, keepdims=True)
    probs_low = probabilities.astype(jnp.bfloat16)
    attn_out = jnp.einsum(
        "grte,egd->tgrd", probs_low, value_three_axes, preferred_element_type=jnp.float32
    )
    row_delta = jnp.sum(gradient_four_axes.astype(jnp.float32) * attn_out, axis=-1)
    grad_probs = jnp.einsum(
        "tgrd,egd->grte", gradient_four_axes, value_three_axes, preferred_element_type=jnp.float32
    )
    grad_scores = probabilities * (grad_probs - jnp.transpose(row_delta, (1, 2, 0))[..., None])
    scores_low = grad_scores.astype(jnp.bfloat16)
    query_gradient = (
        jnp.einsum("grte,egd->tgrd", scores_low, key_three_axes, preferred_element_type=jnp.float32)
        * query_scale
    )
    query_gradient = query_gradient.astype(jnp.bfloat16).reshape(
        shard_length, QUERY_HEADS * HEAD_SIZE
    )
    key_gradient = (
        jnp.einsum(
            "grte,tgrd->egd", scores_low, query_four_axes, preferred_element_type=jnp.float32
        )
        * query_scale
    )
    value_gradient = jnp.einsum(
        "grte,tgrd->egd", probs_low, gradient_four_axes, preferred_element_type=jnp.float32
    )
    return (
        query_gradient,
        key_gradient.reshape(extent_rows, KEY_VALUE_HEADS * HEAD_SIZE),
        value_gradient.reshape(extent_rows, KEY_VALUE_HEADS * HEAD_SIZE),
    )


def shift(x, axis, by):
    count = lax.axis_size(axis)
    pairs = [(i, i + by) for i in range(count) if 0 <= i + by < count]
    return lax.ppermute(x, axis, pairs)


def all_sum(x, axes):
    for axis in axes:
        count = lax.axis_size(axis)
        step = 1
        while step < count:
            x = x + cyclic(x, axis, step)
            step *= 2
    return x


def shards(
    layer_input,
    query_states,
    key_states,
    value_state_rows,
    grad_out,
    segments,
    master,
    first_moment_value,
    second_moment_value,
):
    shard_length = query_states.shape[1]
    kv_width = key_states.shape[2]
    ncx = lax.axis_size("cx")
    icx = lax.axis_index("cx")
    iz = lax.axis_index("cz")
    assert WINDOW // shard_length == 2 * ncx
    block = ctx_index()

    seg_query = segments[0]
    seg_cols = jnp.broadcast_to(seg_query.astype(jnp.bfloat16)[:, None], (shard_length, 128))
    own_kv = jnp.concatenate([key_states[0], value_state_rows[0], seg_cols], axis=1)
    plane_one = shift(own_kv, "cz", 1)
    plane_two = shift(plane_one, "cz", 1)
    slots = [own_kv, plane_one, plane_two]
    sources = [block, block - ncx, block - 2 * ncx]
    wraps = []
    for by in range(1, ncx):
        slots.append(cyclic(plane_one, "cx", by))
        sources.append((iz - 1) * ncx + (icx - by) % ncx)
    for by in range(1, ncx):
        sending_wraps = icx + by >= ncx
        slots.append(cyclic(jnp.where(sending_wraps, plane_two, own_kv), "cx", by))
        got_wrap = icx - by < 0
        wraps.append(sending_wraps)
        sources.append(jnp.where(got_wrap, block - ncx - by, block - by))
    kv_rows = jnp.concatenate(slots, axis=0)
    key_row_block = kv_rows[:, :kv_width]
    value_row_block = kv_rows[:, kv_width : 2 * kv_width]
    seg_key = kv_rows[:, 2 * kv_width]
    index_query = block * shard_length + jnp.arange(shard_length, dtype=jnp.int32)
    index_key = jnp.concatenate(
        [src * shard_length + jnp.arange(shard_length, dtype=jnp.int32) for src in sources]
    )
    query_gradient, key_gradient, value_gradient = attend(
        query_states[0],
        key_row_block,
        value_row_block,
        grad_out[0],
        seg_query.astype(jnp.bfloat16),
        seg_key,
        index_query,
        index_key,
    )
    grads = jnp.concatenate([key_gradient, value_gradient], axis=1)
    slot_grads = [grads[i * shard_length : (i + 1) * shard_length] for i in range(len(slots))]
    low = lambda x: x.astype(jnp.bfloat16)
    own_acc = slot_grads[0]
    one_acc = low(slot_grads[1]).astype(jnp.float32)
    two_acc = low(slot_grads[2]).astype(jnp.float32)
    for k, by in enumerate(range(1, ncx)):
        back = cyclic(low(slot_grads[3 + k]), "cx", -by).astype(jnp.float32)
        one_acc = one_acc + back
    for k, by in enumerate(range(1, ncx)):
        back = cyclic(low(slot_grads[3 + (ncx - 1) + k]), "cx", -by).astype(jnp.float32)
        zero = jnp.zeros_like(back)
        two_acc = two_acc + jnp.where(wraps[k], back, zero)
        own_acc = own_acc + jnp.where(wraps[k], zero, back)
    one_acc = one_acc + shift(low(two_acc), "cz", -1).astype(jnp.float32)
    own_acc = own_acc + shift(low(one_acc), "cz", -1).astype(jnp.float32)
    key_out = own_acc[:, :kv_width].astype(jnp.bfloat16)
    value_out = own_acc[:, kv_width:].astype(jnp.bfloat16)

    nz = lax.axis_size("cz")
    ny = lax.axis_size("y")
    nc = lax.axis_size("core")
    x_own = layer_input[0]
    rows = x_own.shape[1] // (nz * ncx * ny * nc)
    tall = -(-rows // 8) * 8
    x_view = x_own.reshape(shard_length, nz, ncx, ny * nc, rows)
    x_view = jnp.pad(x_view, ((0, 0), (0, 0), (0, 0), (0, 0), (0, tall - rows)))

    def columns(target):
        picked = lax.dynamic_index_in_dim(x_view, target, 2, keepdims=False)
        return picked.reshape(shard_length, nz * ny * nc * tall)

    x_list = [columns(icx)]
    v_list = [value_out]
    for by in range(1, ncx):
        piece = jnp.concatenate([columns((icx + by) % ncx), value_out], axis=1)
        got = cyclic(piece, "cx", by)
        x_list.append(got[:, : -kv_width])
        v_list.append(got[:, -kv_width:])
    partial = lax.dot_general(
        jnp.concatenate(x_list, axis=0),
        jnp.concatenate(v_list, axis=0),
        (((0,), (0,)), ((), ())),
        preferred_element_type=jnp.float32,
    )
    partial = partial.reshape(nz, ny, nc, tall, kv_width)
    icore = lax.axis_index("core")
    stage = lax.dynamic_index_in_dim(partial, icore, 2, keepdims=False)
    for by in range(1, nc):
        sent = lax.dynamic_index_in_dim(partial, (icore + by) % nc, 2, keepdims=False)
        stage = stage + cyclic(low(sent), "core", by).astype(jnp.float32)
    iy = lax.axis_index("y")
    stage_y = lax.dynamic_index_in_dim(stage, iy, 1, keepdims=False)
    for by in range(1, ny):
        sent = lax.dynamic_index_in_dim(stage, (iy + by) % ny, 1, keepdims=False)
        stage_y = stage_y + cyclic(low(sent), "y", by).astype(jnp.float32)
    weight_grad = lax.dynamic_index_in_dim(stage_y, iz, 0, keepdims=False)
    for by in range(1, nz):
        sent = lax.dynamic_index_in_dim(stage_y, (iz + by) % nz, 0, keepdims=False)
        weight_grad = weight_grad + cyclic(sent, "cz", by)

    weight_grad = weight_grad[:rows]
    square_total = lax.psum(jnp.sum(weight_grad * weight_grad), DP)
    square_total = all_sum(square_total, ("cx", "cz"))
    norm_total = jnp.sqrt(square_total + 1e-06)

    ndp = ny * nc
    idp = iy * nc + icore

    def dp_rows(x, axis):
        got = [x] + [cyclic(x, DP, by) for by in range(ndp - 1, 0, -1)]
        rolled = jnp.roll(jnp.stack(got, axis=axis), idp, axis=axis)
        shape = x.shape[:axis] + (ndp * x.shape[axis],) + x.shape[axis + 1 :]
        return rolled.reshape(shape)

    state_all = dp_rows(jnp.stack([master, first_moment_value, second_moment_value]), 1)
    grad_all = dp_rows(weight_grad, 0)
    master_all, first_all, second_all = state_all[0], state_all[1], state_all[2]
    clipped = grad_all * jnp.minimum(1.0, clip_norm / norm_total)
    first_new = beta_first * first_all + (1.0 - beta_first) * clipped
    second_new = beta_second * second_all + (1.0 - beta_second) * clipped * clipped
    step_dir = first_new / correct_first / (jnp.sqrt(second_new / correct_second) + adam_eps)
    master_new = master_all - learn_rate * (step_dir + decay_rate * master_all)
    new_weight = master_new.astype(jnp.bfloat16)
    mine = idp * rows
    new_master = lax.dynamic_slice_in_dim(master_new, mine, rows, 0)
    new_first = lax.dynamic_slice_in_dim(first_new, mine, rows, 0)
    new_second = lax.dynamic_slice_in_dim(second_new, mine, rows, 0)
    return (
        query_gradient[None],
        key_out[None],
        value_out[None],
        new_master,
        new_first,
        new_second,
        new_weight,
    )


def solution(mesh):
    n_ctx = mesh.shape["ctx"]
    n_dp = mesh.shape["dp"]
    z_size = Z_SIZE if n_ctx % Z_SIZE == 0 else n_ctx
    grid = Mesh(
        mesh.devices.reshape(z_size, n_ctx // z_size, n_dp // 2, 2), ("cz", "cx", "y", "core")
    )
    tokens = P(DP, CTX, None)
    owner = P(("cz", "cx", "y", "core"), None)
    return jax.shard_map(
        shards,
        mesh=grid,
        in_specs=(
            tokens,
            tokens,
            tokens,
            tokens,
            tokens,
            P(DP, CTX),
            owner,
            owner,
            owner,
        ),
        out_specs=(
            tokens,
            tokens,
            tokens,
            owner,
            owner,
            owner,
            P(CTX, None),
        ),
        check_vma=False,
    )
```

```python
import jax
import jax.numpy as jnp
from jax import lax
from jax.sharding import Mesh
from jax.sharding import PartitionSpec as P

QUERY_HEADS = 16
KEY_VALUE_HEADS = 8
HEAD_SIZE = 128
WINDOW = 1024
Z_SIZE = 8

CTX = ("cz", "cx")
DP = ("y", "core")

query_scale = 168.0 ** (-0.5)
masked_score = -1e30
clip_norm = 1.0
beta_first = 0.9
beta_second = 0.95
learn_rate = 0.001
decay_rate = 0.1
adam_eps = 1e-08
correct_first = 0.9999734386011124
correct_second = 0.994079470779666


def ctx_size():
    return lax.axis_size("cz") * lax.axis_size("cx")


def ctx_index():
    return lax.axis_index("cz") * lax.axis_size("cx") + lax.axis_index("cx")


def cyclic(x, axis, by):
    count = lax.axis_size(axis)
    return lax.ppermute(x, axis, [(i, (i + by) % count) for i in range(count)])


def attend(
    query_row_block,
    key_row_block,
    value_row_block,
    gradient_rows,
    seg_query,
    seg_key,
    index_query,
    index_key,
):
    shard_length = query_row_block.shape[0]
    extent_rows = key_row_block.shape[0]
    heads_ratio = QUERY_HEADS // KEY_VALUE_HEADS
    query_four_axes = query_row_block.reshape(shard_length, KEY_VALUE_HEADS, heads_ratio, HEAD_SIZE)
    gradient_four_axes = gradient_rows.reshape(
        shard_length, KEY_VALUE_HEADS, heads_ratio, HEAD_SIZE
    )
    key_three_axes = key_row_block.reshape(extent_rows, KEY_VALUE_HEADS, HEAD_SIZE)
    value_three_axes = value_row_block.reshape(extent_rows, KEY_VALUE_HEADS, HEAD_SIZE)
    scores = (
        jnp.einsum(
            "tgrd,egd->grte", query_four_axes, key_three_axes, preferred_element_type=jnp.float32
        )
        * query_scale
    )
    offset = index_query[:, None] - index_key[None, :]
    allowed = (
        (seg_query[:, None] == seg_key[None, :])
        & (offset >= 0)
        & (offset < WINDOW)
        & (index_key[None, :] >= 0)
    )
    scores = jnp.where(allowed, scores, masked_score)
    row_max = jnp.max(scores, axis=-1, keepdims=True)
    weights = jnp.exp(scores - row_max)
    probabilities = weights / jnp.sum(weights, axis=-1, keepdims=True)
    probs_low = probabilities.astype(jnp.bfloat16)
    attn_out = jnp.einsum(
        "grte,egd->tgrd", probs_low, value_three_axes, preferred_element_type=jnp.float32
    )
    row_delta = jnp.sum(gradient_four_axes.astype(jnp.float32) * attn_out, axis=-1)
    grad_probs = jnp.einsum(
        "tgrd,egd->grte", gradient_four_axes, value_three_axes, preferred_element_type=jnp.float32
    )
    grad_scores = probabilities * (grad_probs - jnp.transpose(row_delta, (1, 2, 0))[..., None])
    scores_low = grad_scores.astype(jnp.bfloat16)
    query_gradient = (
        jnp.einsum("grte,egd->tgrd", scores_low, key_three_axes, preferred_element_type=jnp.float32)
        * query_scale
    )
    query_gradient = query_gradient.astype(jnp.bfloat16).reshape(
        shard_length, QUERY_HEADS * HEAD_SIZE
    )
    key_gradient = (
        jnp.einsum(
            "grte,tgrd->egd", scores_low, query_four_axes, preferred_element_type=jnp.float32
        )
        * query_scale
    )
    value_gradient = jnp.einsum(
        "grte,tgrd->egd", probs_low, gradient_four_axes, preferred_element_type=jnp.float32
    )
    return (
        query_gradient,
        key_gradient.reshape(extent_rows, KEY_VALUE_HEADS * HEAD_SIZE),
        value_gradient.reshape(extent_rows, KEY_VALUE_HEADS * HEAD_SIZE),
    )


def shift(x, axis, by):
    count = lax.axis_size(axis)
    pairs = [(i, i + by) for i in range(count) if 0 <= i + by < count]
    return lax.ppermute(x, axis, pairs)


def all_sum(x, axes):
    for axis in axes:
        count = lax.axis_size(axis)
        step = 1
        while step < count:
            x = x + cyclic(x, axis, step)
            step *= 2
    return x


def shards(
    layer_input,
    query_states,
    key_states,
    value_state_rows,
    grad_out,
    segments,
    master,
    first_moment_value,
    second_moment_value,
):
    shard_length = query_states.shape[1]
    kv_width = key_states.shape[2]
    ncx = lax.axis_size("cx")
    icx = lax.axis_index("cx")
    iz = lax.axis_index("cz")
    assert WINDOW // shard_length == 2 * ncx
    block = ctx_index()

    seg_query = segments[0]
    seg_cols = jnp.broadcast_to(seg_query.astype(jnp.bfloat16)[:, None], (shard_length, 128))
    own_kv = jnp.concatenate([key_states[0], value_state_rows[0], seg_cols], axis=1)
    plane_one = shift(own_kv, "cz", 1)
    plane_two = shift(plane_one, "cz", 1)
    slots = [own_kv, plane_one, plane_two]
    sources = [block, block - ncx, block - 2 * ncx]
    wraps = []
    for by in range(1, ncx):
        slots.append(cyclic(plane_one, "cx", by))
        sources.append((iz - 1) * ncx + (icx - by) % ncx)
    for by in range(1, ncx):
        sending_wraps = icx + by >= ncx
        slots.append(cyclic(jnp.where(sending_wraps, plane_two, own_kv), "cx", by))
        got_wrap = icx - by < 0
        wraps.append(sending_wraps)
        sources.append(jnp.where(got_wrap, block - ncx - by, block - by))
    kv_rows = jnp.concatenate(slots, axis=0)
    key_row_block = kv_rows[:, :kv_width]
    value_row_block = kv_rows[:, kv_width : 2 * kv_width]
    seg_key = kv_rows[:, 2 * kv_width]
    index_query = block * shard_length + jnp.arange(shard_length, dtype=jnp.int32)
    index_key = jnp.concatenate(
        [src * shard_length + jnp.arange(shard_length, dtype=jnp.int32) for src in sources]
    )
    query_gradient, key_gradient, value_gradient = attend(
        query_states[0],
        key_row_block,
        value_row_block,
        grad_out[0],
        seg_query.astype(jnp.bfloat16),
        seg_key,
        index_query,
        index_key,
    )
    grads = jnp.concatenate([key_gradient, value_gradient], axis=1)
    slot_grads = [grads[i * shard_length : (i + 1) * shard_length] for i in range(len(slots))]
    low = lambda x: x.astype(jnp.bfloat16)
    own_acc = slot_grads[0]
    one_acc = low(slot_grads[1]).astype(jnp.float32)
    two_acc = low(slot_grads[2]).astype(jnp.float32)
    for k, by in enumerate(range(1, ncx)):
        back = cyclic(low(slot_grads[3 + k]), "cx", -by).astype(jnp.float32)
        one_acc = one_acc + back
    for k, by in enumerate(range(1, ncx)):
        back = cyclic(low(slot_grads[3 + (ncx - 1) + k]), "cx", -by).astype(jnp.float32)
        zero = jnp.zeros_like(back)
        two_acc = two_acc + jnp.where(wraps[k], back, zero)
        own_acc = own_acc + jnp.where(wraps[k], zero, back)
    one_acc = one_acc + shift(low(two_acc), "cz", -1).astype(jnp.float32)
    own_acc = own_acc + shift(low(one_acc), "cz", -1).astype(jnp.float32)
    key_out = own_acc[:, :kv_width].astype(jnp.bfloat16)
    value_out = own_acc[:, kv_width:].astype(jnp.bfloat16)

    nz = lax.axis_size("cz")
    ny = lax.axis_size("y")
    nc = lax.axis_size("core")
    x_own = layer_input[0]
    rows = x_own.shape[1] // (nz * ncx * ny * nc)
    tall = -(-rows // 8) * 8
    x_view = x_own.reshape(shard_length, nz, ncx, ny * nc, rows)
    x_view = jnp.pad(x_view, ((0, 0), (0, 0), (0, 0), (0, 0), (0, tall - rows)))

    def columns(target):
        picked = lax.dynamic_index_in_dim(x_view, target, 2, keepdims=False)
        return picked.reshape(shard_length, nz * ny * nc * tall)

    x_list = [columns(icx)]
    v_list = [value_out]
    landed = (kv_rows[0, 0] * 0).astype(x_own.dtype)
    for by in range(1, ncx):
        x_list.append(cyclic(columns((icx + by) % ncx) + landed, "cx", by))
        v_list.append(cyclic(value_out, "cx", by))
    partial = lax.dot_general(
        jnp.concatenate(x_list, axis=0),
        jnp.concatenate(v_list, axis=0),
        (((0,), (0,)), ((), ())),
        preferred_element_type=jnp.float32,
    )
    partial = partial.reshape(nz, ny, nc, tall, kv_width)
    icore = lax.axis_index("core")
    stage = lax.dynamic_index_in_dim(partial, icore, 2, keepdims=False)
    for by in range(1, nc):
        sent = lax.dynamic_index_in_dim(partial, (icore + by) % nc, 2, keepdims=False)
        stage = stage + cyclic(low(sent), "core", by).astype(jnp.float32)
    iy = lax.axis_index("y")
    stage_y = lax.dynamic_index_in_dim(stage, iy, 1, keepdims=False)
    for by in range(1, ny):
        sent = lax.dynamic_index_in_dim(stage, (iy + by) % ny, 1, keepdims=False)
        stage_y = stage_y + cyclic(low(sent), "y", by).astype(jnp.float32)
    weight_grad = lax.dynamic_index_in_dim(stage_y, iz, 0, keepdims=False)
    for by in range(1, nz):
        sent = lax.dynamic_index_in_dim(stage_y, (iz + by) % nz, 0, keepdims=False)
        weight_grad = weight_grad + cyclic(sent, "cz", by)

    weight_grad = weight_grad[:rows]
    square_total = lax.psum(jnp.sum(weight_grad * weight_grad), DP)
    square_total = all_sum(square_total, ("cx", "cz"))
    norm_total = jnp.sqrt(square_total + 1e-06)
    clipped = weight_grad * jnp.minimum(1.0, clip_norm / norm_total)
    new_first = beta_first * first_moment_value + (1.0 - beta_first) * clipped
    new_second = beta_second * second_moment_value + (1.0 - beta_second) * clipped * clipped
    step_dir = new_first / correct_first / (jnp.sqrt(new_second / correct_second) + adam_eps)
    new_master = master - learn_rate * (step_dir + decay_rate * master)
    new_weight = lax.all_gather(new_master.astype(jnp.bfloat16), DP, axis=0, tiled=True)
    return (
        query_gradient[None],
        key_out[None],
        value_out[None],
        new_master,
        new_first,
        new_second,
        new_weight,
    )


def solution(mesh):
    n_ctx = mesh.shape["ctx"]
    n_dp = mesh.shape["dp"]
    z_size = Z_SIZE if n_ctx % Z_SIZE == 0 else n_ctx
    grid = Mesh(
        mesh.devices.reshape(z_size, n_ctx // z_size, n_dp // 2, 2), ("cz", "cx", "y", "core")
    )
    tokens = P(DP, CTX, None)
    owner = P(("cz", "cx", "y", "core"), None)
    return jax.shard_map(
        shards,
        mesh=grid,
        in_specs=(
            tokens,
            tokens,
            tokens,
            tokens,
            tokens,
            P(DP, CTX),
            owner,
            owner,
            owner,
        ),
        out_specs=(
            tokens,
            tokens,
            tokens,
            owner,
            owner,
            owner,
            P(CTX, None),
        ),
        check_vma=False,
    )
```

```python
import jax
import jax.numpy as jnp
from jax import lax
from jax.sharding import Mesh
from jax.sharding import PartitionSpec as P

QUERY_HEADS = 16
KEY_VALUE_HEADS = 8
HEAD_SIZE = 128
WINDOW = 1024
Z_SIZE = 8

CTX = ("cz", "cx")
DP = ("y", "core")

query_scale = 168.0 ** (-0.5)
masked_score = -1e30
clip_norm = 1.0
beta_first = 0.9
beta_second = 0.95
learn_rate = 0.001
decay_rate = 0.1
adam_eps = 1e-08
correct_first = 0.9999734386011124
correct_second = 0.994079470779666


def ctx_size():
    return lax.axis_size("cz") * lax.axis_size("cx")


def ctx_index():
    return lax.axis_index("cz") * lax.axis_size("cx") + lax.axis_index("cx")


def cyclic(x, axis, by):
    count = lax.axis_size(axis)
    return lax.ppermute(x, axis, [(i, (i + by) % count) for i in range(count)])


def attend(
    query_row_block,
    key_row_block,
    value_row_block,
    gradient_rows,
    seg_query,
    seg_key,
    index_query,
    index_key,
):
    shard_length = query_row_block.shape[0]
    extent_rows = key_row_block.shape[0]
    heads_ratio = QUERY_HEADS // KEY_VALUE_HEADS
    query_four_axes = query_row_block.reshape(shard_length, KEY_VALUE_HEADS, heads_ratio, HEAD_SIZE)
    gradient_four_axes = gradient_rows.reshape(
        shard_length, KEY_VALUE_HEADS, heads_ratio, HEAD_SIZE
    )
    key_three_axes = key_row_block.reshape(extent_rows, KEY_VALUE_HEADS, HEAD_SIZE)
    value_three_axes = value_row_block.reshape(extent_rows, KEY_VALUE_HEADS, HEAD_SIZE)
    scores = (
        jnp.einsum(
            "tgrd,egd->grte", query_four_axes, key_three_axes, preferred_element_type=jnp.float32
        )
        * query_scale
    )
    offset = index_query[:, None] - index_key[None, :]
    allowed = (
        (seg_query[:, None] == seg_key[None, :])
        & (offset >= 0)
        & (offset < WINDOW)
        & (index_key[None, :] >= 0)
    )
    scores = jnp.where(allowed, scores, masked_score)
    row_max = jnp.max(scores, axis=-1, keepdims=True)
    weights = jnp.exp(scores - row_max)
    probabilities = weights / jnp.sum(weights, axis=-1, keepdims=True)
    probs_low = probabilities.astype(jnp.bfloat16)
    attn_out = jnp.einsum(
        "grte,egd->tgrd", probs_low, value_three_axes, preferred_element_type=jnp.float32
    )
    row_delta = jnp.sum(gradient_four_axes.astype(jnp.float32) * attn_out, axis=-1)
    grad_probs = jnp.einsum(
        "tgrd,egd->grte", gradient_four_axes, value_three_axes, preferred_element_type=jnp.float32
    )
    grad_scores = probabilities * (grad_probs - jnp.transpose(row_delta, (1, 2, 0))[..., None])
    scores_low = grad_scores.astype(jnp.bfloat16)
    query_gradient = (
        jnp.einsum("grte,egd->tgrd", scores_low, key_three_axes, preferred_element_type=jnp.float32)
        * query_scale
    )
    query_gradient = query_gradient.astype(jnp.bfloat16).reshape(
        shard_length, QUERY_HEADS * HEAD_SIZE
    )
    key_gradient = (
        jnp.einsum(
            "grte,tgrd->egd", scores_low, query_four_axes, preferred_element_type=jnp.float32
        )
        * query_scale
    )
    value_gradient = jnp.einsum(
        "grte,tgrd->egd", probs_low, gradient_four_axes, preferred_element_type=jnp.float32
    )
    return (
        query_gradient,
        key_gradient.reshape(extent_rows, KEY_VALUE_HEADS * HEAD_SIZE),
        value_gradient.reshape(extent_rows, KEY_VALUE_HEADS * HEAD_SIZE),
    )


def shift(x, axis, by):
    count = lax.axis_size(axis)
    pairs = [(i, i + by) for i in range(count) if 0 <= i + by < count]
    return lax.ppermute(x, axis, pairs)


def all_sum(x, axes):
    for axis in axes:
        count = lax.axis_size(axis)
        step = 1
        while step < count:
            x = x + cyclic(x, axis, step)
            step *= 2
    return x


def shards(
    layer_input,
    query_states,
    key_states,
    value_state_rows,
    grad_out,
    segments,
    master,
    first_moment_value,
    second_moment_value,
):
    shard_length = query_states.shape[1]
    kv_width = key_states.shape[2]
    ncx = lax.axis_size("cx")
    icx = lax.axis_index("cx")
    iz = lax.axis_index("cz")
    assert WINDOW // shard_length == 2 * ncx
    block = ctx_index()

    seg_query = segments[0]
    seg_cols = jnp.broadcast_to(seg_query.astype(jnp.bfloat16)[:, None], (shard_length, 128))
    own_kv = jnp.concatenate([key_states[0], value_state_rows[0], seg_cols], axis=1)
    plane_one = shift(own_kv, "cz", 1)
    plane_two = shift(plane_one, "cz", 1)
    slots = [own_kv, plane_one, plane_two]
    sources = [block, block - ncx, block - 2 * ncx]
    wraps = []
    for by in range(1, ncx):
        slots.append(cyclic(plane_one, "cx", by))
        sources.append((iz - 1) * ncx + (icx - by) % ncx)
    for by in range(1, ncx):
        sending_wraps = icx + by >= ncx
        slots.append(cyclic(jnp.where(sending_wraps, plane_two, own_kv), "cx", by))
        got_wrap = icx - by < 0
        wraps.append(sending_wraps)
        sources.append(jnp.where(got_wrap, block - ncx - by, block - by))
    kv_rows = jnp.concatenate(slots, axis=0)
    key_row_block = kv_rows[:, :kv_width]
    value_row_block = kv_rows[:, kv_width : 2 * kv_width]
    seg_key = kv_rows[:, 2 * kv_width]
    index_query = block * shard_length + jnp.arange(shard_length, dtype=jnp.int32)
    index_key = jnp.concatenate(
        [src * shard_length + jnp.arange(shard_length, dtype=jnp.int32) for src in sources]
    )
    query_gradient, key_gradient, value_gradient = attend(
        query_states[0],
        key_row_block,
        value_row_block,
        grad_out[0],
        seg_query.astype(jnp.bfloat16),
        seg_key,
        index_query,
        index_key,
    )
    grads = jnp.concatenate([key_gradient, value_gradient], axis=1)
    slot_grads = [grads[i * shard_length : (i + 1) * shard_length] for i in range(len(slots))]
    low = lambda x: x.astype(jnp.bfloat16)
    own_acc = slot_grads[0]
    one_acc = low(slot_grads[1]).astype(jnp.float32)
    two_acc = low(slot_grads[2]).astype(jnp.float32)
    for k, by in enumerate(range(1, ncx)):
        back = cyclic(low(slot_grads[3 + k]), "cx", -by).astype(jnp.float32)
        one_acc = one_acc + back
    for k, by in enumerate(range(1, ncx)):
        back = cyclic(low(slot_grads[3 + (ncx - 1) + k]), "cx", -by).astype(jnp.float32)
        zero = jnp.zeros_like(back)
        two_acc = two_acc + jnp.where(wraps[k], back, zero)
        own_acc = own_acc + jnp.where(wraps[k], zero, back)
    one_acc = one_acc + shift(low(two_acc), "cz", -1).astype(jnp.float32)
    own_acc = own_acc + shift(low(one_acc), "cz", -1).astype(jnp.float32)
    key_out = own_acc[:, :kv_width].astype(jnp.bfloat16)
    value_out = own_acc[:, kv_width:].astype(jnp.bfloat16)

    nz = lax.axis_size("cz")
    ny = lax.axis_size("y")
    nc = lax.axis_size("core")
    x_own = layer_input[0]
    rows = x_own.shape[1] // (nz * ncx * ny * nc)
    tall = -(-rows // 8) * 8
    x_view = x_own.reshape(shard_length, nz, ncx, ny * nc, rows)
    x_view = jnp.pad(x_view, ((0, 0), (0, 0), (0, 0), (0, 0), (0, tall - rows)))

    def columns(target):
        picked = lax.dynamic_index_in_dim(x_view, target, 2, keepdims=False)
        return picked.reshape(shard_length, nz * ny * nc * tall)

    x_list = [columns(icx)]
    v_list = [value_out]
    for by in range(1, ncx):
        piece = jnp.concatenate([columns((icx + by) % ncx), value_out], axis=1)
        got = cyclic(piece, "cx", by)
        x_list.append(got[:, : -kv_width])
        v_list.append(got[:, -kv_width:])
    partial = lax.dot_general(
        jnp.concatenate(x_list, axis=0),
        jnp.concatenate(v_list, axis=0),
        (((0,), (0,)), ((), ())),
        preferred_element_type=jnp.float32,
    )
    partial = partial.reshape(nz, ny, nc, tall, kv_width)
    icore = lax.axis_index("core")
    stage = lax.dynamic_index_in_dim(partial, icore, 2, keepdims=False)
    for by in range(1, nc):
        sent = lax.dynamic_index_in_dim(partial, (icore + by) % nc, 2, keepdims=False)
        stage = stage + cyclic(low(sent), "core", by).astype(jnp.float32)
    iy = lax.axis_index("y")
    stage_y = lax.dynamic_index_in_dim(stage, iy, 1, keepdims=False)
    for by in range(1, ny):
        sent = lax.dynamic_index_in_dim(stage, (iy + by) % ny, 1, keepdims=False)
        stage_y = stage_y + cyclic(low(sent), "y", by).astype(jnp.float32)
    weight_grad = lax.dynamic_index_in_dim(stage_y, iz, 0, keepdims=False)
    for by in range(1, nz):
        sent = lax.dynamic_index_in_dim(stage_y, (iz + by) % nz, 0, keepdims=False)
        weight_grad = weight_grad + cyclic(sent, "cz", by)

    weight_grad = weight_grad[:rows]
    square_total = lax.psum(jnp.sum(weight_grad * weight_grad), ("cx", "y", "core"))
    square_total = all_sum(square_total, ("cz",))
    norm_total = jnp.sqrt(square_total + 1e-06)
    clipped = weight_grad * jnp.minimum(1.0, clip_norm / norm_total)
    new_first = beta_first * first_moment_value + (1.0 - beta_first) * clipped
    new_second = beta_second * second_moment_value + (1.0 - beta_second) * clipped * clipped
    step_dir = new_first / correct_first / (jnp.sqrt(new_second / correct_second) + adam_eps)
    new_master = master - learn_rate * (step_dir + decay_rate * master)
    new_weight = lax.all_gather(new_master.astype(jnp.bfloat16), DP, axis=0, tiled=True)
    return (
        query_gradient[None],
        key_out[None],
        value_out[None],
        new_master,
        new_first,
        new_second,
        new_weight,
    )


def solution(mesh):
    n_ctx = mesh.shape["ctx"]
    n_dp = mesh.shape["dp"]
    z_size = Z_SIZE if n_ctx % Z_SIZE == 0 else n_ctx
    grid = Mesh(
        mesh.devices.reshape(z_size, n_ctx // z_size, n_dp // 2, 2), ("cz", "cx", "y", "core")
    )
    tokens = P(DP, CTX, None)
    owner = P(("cz", "cx", "y", "core"), None)
    return jax.shard_map(
        shards,
        mesh=grid,
        in_specs=(
            tokens,
            tokens,
            tokens,
            tokens,
            tokens,
            P(DP, CTX),
            owner,
            owner,
            owner,
        ),
        out_specs=(
            tokens,
            tokens,
            tokens,
            owner,
            owner,
            owner,
            P(CTX, None),
        ),
        check_vma=False,
    )
```
